32 devices in a mesh: segment: 4 (over x, core), fsdp: 8 (over z, y).
Axes of the slice: x: 2, y: 2, z: 4, core: 2. Of those that a mesh axis runs over, the one named last changes fastest.
Arguments:
- latents: float32 [2, 8, 25, 4, 5, 320], P(None, 'fsdp'), may hold values from -6 to 6
- spatial_weight: float32 [4, 2880, 320], P('segment', 'fsdp'), may hold values from -0.109375 to 0.109375
- temporal_weight: float32 [4, 960, 320], P('segment', 'fsdp'), may hold values from -0.1875 to 0.1875
- skip_weight: float32 [4, 320, 320], P('segment', 'fsdp'), may hold values from -0.3125 to 0.3125
- norm_gain: float32 [4, 2, 320], P('segment'), may hold values from 0.25 to 1.75
- norm_bias: float32 [4, 2, 320], P('segment'), may hold values from -3 to 3
Outputs:
- section_out: float32 [4, 2, 8, 25, 4, 5, 320], P('segment', None, 'fsdp')
The draws below stay inside these ranges and needn't reach their ends.
All inputs are finite; a program needn't handle non-finite values.
Results may differ from the reference program's by a relative error of at most 0.0003.
Values sent between devices are 32-bit elements; how exact they have to be, the bound alone decides.
No kernel may reach another device: no remote copies, remote signals or barrier semaphores. Data moves between devices by JAX's collectives and lax.ppermute only.
A program may use at most 128 MiB of HBM per device.

```python
import jax
import jax.numpy as jnp
from jax import lax

C = 320
GROUPS = 32
FRAMES = 25
ROWS = 4
COLS = 5
MICRO = 2
SAMPLES = 8
N_SEGMENT = 4


def steps_of(own_key, shape, shards, least, largest):
    level = 1.0
    for dim, parts in shards:
        heights = jax.random.uniform(jax.random.fold_in(jax.random.fold_in(own_key, 6), dim), (parts,), jnp.float32, least / len(shards), largest / len(shards))
        level = level * jnp.repeat(jnp.exp(heights), shape[dim] // parts).reshape((-1,) + (1,) * (len(shape) - 1 - dim))
    return level


def gaussian(own_key, extent, scale, bound, shards=(), dtype=jnp.bfloat16):
    entries = scale * jax.random.normal(own_key, extent, jnp.float32)
    if shards:
        entries = entries * steps_of(own_key, extent, shards, -0.22, 0.18)
    return jnp.clip(entries, -bound, bound).astype(dtype)


def setup_inputs(seed: int = 0) -> dict:
    streams_of = jax.random.split(jax.random.key(seed), 7)
    return {
        "latents": gaussian(streams_of[0], (MICRO, SAMPLES, FRAMES, ROWS, COLS, C), 1.0, 6.0, ((1, 8),), jnp.float32),
        "spatial_weight": gaussian(streams_of[1], (N_SEGMENT, 9 * C, C), (9 * C) ** -0.5, 0.109375, ((0, 4), (1, 8)), jnp.float32),
        "temporal_weight": gaussian(streams_of[2], (N_SEGMENT, 3 * C, C), (3 * C) ** -0.5, 0.1875, ((0, 4), (1, 8)), jnp.float32),
        "skip_weight": gaussian(streams_of[3], (N_SEGMENT, C, C), C ** -0.5, 0.3125, ((0, 4), (1, 8)), jnp.float32),
        "norm_gain": jnp.clip(1.0 + 0.15 * jax.random.normal(streams_of[4], (N_SEGMENT, 2, C), jnp.float32), 0.25, 1.75),
        "norm_bias": gaussian(streams_of[5], (N_SEGMENT, 2, C), 0.5, 3.0, ((0, 4),), jnp.float32),
    }


highest = lax.Precision.HIGHEST

def matmul_last(field, matrix):
    flat = field.reshape(-1, field.shape[-1])
    result = jnp.dot(flat, matrix, precision=highest, preferred_element_type=jnp.float32)
    return result.reshape(field.shape[:-1] + (matrix.shape[1],))

def group_norm(field, gain, offset):
    shape = field.shape
    width = shape[-1]
    grouped = field.reshape(shape[0], -1, GROUPS, width // GROUPS)
    center = lax.optimization_barrier(jnp.mean(grouped, axis=(1, 3), keepdims=True))
    spread = lax.optimization_barrier(jnp.mean((grouped - center) ** 2, axis=(1, 3), keepdims=True))
    normed = ((grouped - center) * lax.rsqrt(spread + 1e-05)).reshape(shape)
    return normed * gain + offset

def spatial_patches(field):
    padded = jnp.pad(field, ((0, 0), (0, 0), (1, 1), (1, 1), (0, 0)))
    rows, cols = (field.shape[2], field.shape[3])
    pieces = []
    for delta_row in range(3):
        for delta_col in range(3):
            pieces.append(padded[:, :, delta_row:delta_row + rows, delta_col:delta_col + cols, :])
    return jnp.concatenate(pieces, axis=-1)

def temporal_patches(field):
    padded = jnp.pad(field, ((0, 0), (1, 1), (0, 0), (0, 0), (0, 0)))
    frames = field.shape[1]
    return jnp.concatenate([padded[:, 0:frames], padded[:, 1:frames + 1], padded[:, 2:frames + 2]], axis=-1)

def section(stream, skip_in, spatial, temporal, skip_mat, gains, offsets):
    hidden = stream + matmul_last(skip_in, skip_mat)
    first = jax.nn.silu(group_norm(hidden, gains[0], offsets[0]))
    mixed = hidden + matmul_last(spatial_patches(first), spatial)
    second = jax.nn.silu(group_norm(mixed, gains[1], offsets[1]))
    return mixed + matmul_last(temporal_patches(second), temporal)

def reference(latents, spatial_weight, temporal_weight, skip_weight, norm_gain, norm_bias):
    results = []
    for segment_index in range(N_SEGMENT):
        results.append([None] * MICRO)
    for micro_index in range(MICRO):
        stream = latents[micro_index]
        for segment_index in range(N_SEGMENT):
            if segment_index == N_SEGMENT - 1:
                skip_in = results[0][micro_index]
            else:
                skip_in = jnp.zeros_like(stream)
            stream = section(stream, skip_in, spatial_weight[segment_index], temporal_weight[segment_index], skip_weight[segment_index], norm_gain[segment_index], norm_bias[segment_index])
            results[segment_index][micro_index] = stream
    return jnp.stack([jnp.stack(row) for row in results])
```

```python
import jax
import jax.numpy as jnp
from jax import lax
from jax.sharding import PartitionSpec as P

GROUPS = 32
MICRO = 2


precise = lax.Precision.HIGH


def from_behind(shard, axis, by):
    size = lax.axis_size(axis)
    pairs = [(i, i + by) for i in range(size) if 0 <= i + by < size]
    return lax.ppermute(shard, axis, pairs)


def group_norm(field, samples, gain, offset):
    width = field.shape[-1]
    grouped = field.reshape(samples, -1, GROUPS, width // GROUPS)
    center = jnp.mean(grouped, axis=(1, 3), keepdims=True)
    spread = jnp.mean((grouped - center) ** 2, axis=(1, 3), keepdims=True)
    normed = ((grouped - center) * lax.rsqrt(spread + 1e-05)).reshape(field.shape)
    return normed * gain + offset


def shifted(field, offset, valid, pad):
    padded = jnp.pad(field, ((pad, pad), (0, 0)))
    rows = field.shape[0]
    piece = padded[pad + offset : pad + offset + rows]
    return jnp.where(valid, piece, jnp.zeros_like(piece))


def spatial_conv(first, spatial3, frames, rows, cols):
    positions = first.shape[0]
    pos = lax.broadcasted_iota(jnp.int32, (positions, 1), 0)
    within = pos % (rows * cols)
    row = within // cols
    col = within % cols
    pieces = []
    for delta_row in range(3):
        for delta_col in range(3):
            r = row + delta_row - 1
            c = col + delta_col - 1
            valid = (r >= 0) & (r < rows) & (c >= 0) & (c < cols)
            offset = (delta_row - 1) * cols + (delta_col - 1)
            pieces.append(shifted(first, offset, valid, cols + 1))
    stack = jnp.stack(pieces, axis=0)
    return jnp.einsum(
        "tpc,tco->po", stack, spatial3, precision=precise, preferred_element_type=jnp.float32
    )


def temporal_conv(second, temporal3, frames, rows, cols):
    positions = second.shape[0]
    plane = rows * cols
    pos = lax.broadcasted_iota(jnp.int32, (positions, 1), 0)
    frame = (pos // plane) % frames
    pieces = []
    for tap in range(3):
        f = frame + tap - 1
        valid = (f >= 0) & (f < frames)
        pieces.append(shifted(second, (tap - 1) * plane, valid, plane))
    stack = jnp.stack(pieces, axis=0)
    return jnp.einsum(
        "tpc,tco->po", stack, temporal3, precision=precise, preferred_element_type=jnp.float32
    )


def section(stream, skip_in, spatial3, temporal3, skip_mat, gains, offsets):
    samples, frames, rows, cols, width = stream.shape
    x = stream.reshape(-1, width)
    if skip_in is None:
        hidden = x
    else:
        hidden = x + jnp.dot(
            skip_in.reshape(-1, width), skip_mat, precision=precise,
            preferred_element_type=jnp.float32,
        )
    first = jax.nn.silu(group_norm(hidden, samples, gains[0], offsets[0]))
    mixed = hidden + spatial_conv(first, spatial3, frames, rows, cols)
    second = jax.nn.silu(group_norm(mixed, samples, gains[1], offsets[1]))
    out = mixed + temporal_conv(second, temporal3, frames, rows, cols)
    return out.reshape(stream.shape)


def per_device(latents, spatial_weight, temporal_weight, skip_weight, norm_gain, norm_bias):
    sections = lax.axis_size("segment")
    position = lax.axis_index("segment")
    steps_total = MICRO + sections - 1
    gains = norm_gain[0]
    offsets = norm_bias[0]
    width = spatial_weight.shape[-1]
    rs, rt = spatial_weight.shape[1], temporal_weight.shape[1]
    pack = jnp.concatenate([spatial_weight[0], temporal_weight[0], skip_weight[0]], axis=0)
    gathered = lax.all_gather(pack, "fsdp", axis=0, tiled=False)
    spatial3 = gathered[:, :rs].reshape(9, width, width)
    temporal3 = gathered[:, rs : rs + rt].reshape(3, width, width)
    skip_mat = gathered[:, rs + rt :].reshape(width, width)
    blank = jnp.zeros_like(latents[0])
    results = [blank] * MICRO
    previous = blank
    for moment in range(steps_total):
        if moment == 0:
            incoming = blank
        else:
            incoming = from_behind(previous, "segment", 1)
        fresh = latents[min(moment, MICRO - 1)] if moment < MICRO else blank
        stream = jnp.where(position == 0, fresh, incoming)
        late_index = moment - (sections - 1)
        skip_in = None
        if 0 <= late_index < MICRO:
            skip_in = from_behind(results[late_index], "segment", sections - 1)
        output = section(stream, skip_in, spatial3, temporal3, skip_mat, gains, offsets)
        which = moment - position
        for slot_index in range(MICRO):
            results[slot_index] = jnp.where(which == slot_index, output, results[slot_index])
        previous = output
    return jnp.stack(results)[None]


def solution(mesh):
    placed = (
        P(None, "fsdp", None, None, None, None),
        P("segment", "fsdp", None),
        P("segment", "fsdp", None),
        P("segment", "fsdp", None),
        P("segment", None, None),
        P("segment", None, None),
    )
    return jax.shard_map(
        per_device,
        mesh=mesh,
        in_specs=placed,
        out_specs=P("segment", None, "fsdp", None, None, None, None),
        check_vma=False,
    )
```

```python
import jax
import jax.numpy as jnp
from jax import lax
from jax.sharding import PartitionSpec as P

GROUPS = 32
MICRO = 2


precise = lax.Precision.HIGH


def from_behind(shard, axis, by):
    size = lax.axis_size(axis)
    pairs = [(i, i + by) for i in range(size) if 0 <= i + by < size]
    return lax.ppermute(shard, axis, pairs)


def group_norm(field, samples, gain, offset):
    width = field.shape[-1]
    grouped = field.reshape(samples, -1, GROUPS, width // GROUPS)
    center = jnp.mean(grouped, axis=(1, 3), keepdims=True)
    spread = jnp.mean((grouped - center) ** 2, axis=(1, 3), keepdims=True)
    normed = ((grouped - center) * lax.rsqrt(spread + 1e-05)).reshape(field.shape)
    return normed * gain + offset


def shifted(field, offset, valid, pad):
    padded = jnp.pad(field, ((pad, pad), (0, 0)))
    rows = field.shape[0]
    piece = padded[pad + offset : pad + offset + rows]
    return jnp.where(valid, piece, jnp.zeros_like(piece))


def spatial_conv(first, spatial3, frames, rows, cols):
    positions = first.shape[0]
    products = jnp.einsum(
        "pc,tco->tpo", first, spatial3, precision=precise, preferred_element_type=jnp.float32
    )
    pos = lax.broadcasted_iota(jnp.int32, (positions, 1), 0)
    within = pos % (rows * cols)
    row = within // cols
    col = within % cols
    total = None
    for delta_row in range(3):
        for delta_col in range(3):
            r = row + delta_row - 1
            c = col + delta_col - 1
            valid = (r >= 0) & (r < rows) & (c >= 0) & (c < cols)
            offset = (delta_row - 1) * cols + (delta_col - 1)
            piece = shifted(products[3 * delta_row + delta_col], offset, valid, cols + 1)
            total = piece if total is None else total + piece
    return total


def temporal_conv(second, temporal3, frames, rows, cols):
    positions = second.shape[0]
    plane = rows * cols
    products = jnp.einsum(
        "pc,tco->tpo", second, temporal3, precision=precise, preferred_element_type=jnp.float32
    )
    pos = lax.broadcasted_iota(jnp.int32, (positions, 1), 0)
    frame = (pos // plane) % frames
    total = None
    for tap in range(3):
        f = frame + tap - 1
        valid = (f >= 0) & (f < frames)
        piece = shifted(products[tap], (tap - 1) * plane, valid, plane)
        total = piece if total is None else total + piece
    return total


def section(x, skip_in, spatial3, temporal3, skip_mat, gains, offsets, dims):
    samples, frames, rows, cols = dims
    if skip_in is None:
        hidden = x
    else:
        hidden = x + jnp.dot(
            skip_in, skip_mat, precision=precise, preferred_element_type=jnp.float32
        )
    first = jax.nn.silu(group_norm(hidden, samples, gains[0], offsets[0]))
    mixed = hidden + spatial_conv(first, spatial3, frames, rows, cols)
    second = jax.nn.silu(group_norm(mixed, samples, gains[1], offsets[1]))
    return mixed + temporal_conv(second, temporal3, frames, rows, cols)


def gather_rows(pack, axis):
    size = lax.axis_size(axis)
    if size > 8:
        return lax.all_gather(pack, axis, axis=0, tiled=False)
    me = lax.axis_index(axis)
    out = jnp.zeros((size,) + pack.shape, pack.dtype)
    out = lax.dynamic_update_index_in_dim(out, pack, me, 0)
    for k in range(1, size):
        got = lax.ppermute(pack, axis, [(i, (i + k) % size) for i in range(size)])
        out = lax.dynamic_update_index_in_dim(out, got, (me + size - k) % size, 0)
    return out


def per_device(latents, spatial_weight, temporal_weight, skip_weight, norm_gain, norm_bias):
    sections = lax.axis_size("segment")
    position = lax.axis_index("segment")
    steps_total = MICRO + sections - 1
    gains = norm_gain[0]
    offsets = norm_bias[0]
    width = spatial_weight.shape[-1]
    micro, samples, frames, rows, cols = latents.shape[:5]
    dims = (samples, frames, rows, cols)
    flat = latents.reshape(micro, -1, width)
    rs, rt = spatial_weight.shape[1], temporal_weight.shape[1]
    pack = jnp.concatenate([spatial_weight[0], temporal_weight[0], skip_weight[0]], axis=0)
    gathered = gather_rows(pack, "fsdp")
    spatial3 = gathered[:, :rs].reshape(9, width, width)
    temporal3 = gathered[:, rs : rs + rt].reshape(3, width, width)
    skip_mat = gathered[:, rs + rt :].reshape(width, width)
    blank = jnp.zeros_like(flat[0])
    results = [blank] * MICRO
    previous = blank
    for moment in range(steps_total):
        if moment == 0:
            incoming = blank
        else:
            incoming = from_behind(previous, "segment", 1)
        fresh = flat[min(moment, MICRO - 1)] if moment < MICRO else blank
        stream = jnp.where(position == 0, fresh, incoming)
        late_index = moment - (sections - 1)
        skip_in = None
        if 0 <= late_index < MICRO:
            skip_in = from_behind(results[late_index], "segment", sections - 1)
        output = section(stream, skip_in, spatial3, temporal3, skip_mat, gains, offsets, dims)
        which = moment - position
        for slot_index in range(MICRO):
            results[slot_index] = jnp.where(which == slot_index, output, results[slot_index])
        previous = output
    return jnp.stack(results).reshape((1,) + latents.shape)


def solution(mesh):
    placed = (
        P(None, "fsdp", None, None, None, None),
        P("segment", "fsdp", None),
        P("segment", "fsdp", None),
        P("segment", "fsdp", None),
        P("segment", None, None),
        P("segment", None, None),
    )
    return jax.shard_map(
        per_device,
        mesh=mesh,
        in_specs=placed,
        out_specs=P("segment", None, "fsdp", None, None, None, None),
        check_vma=False,
    )
```

```python
import jax
import jax.numpy as jnp
from jax import lax
from jax.sharding import PartitionSpec as P

GROUPS = 32
MICRO = 2


precise = lax.Precision.HIGH


def group_norm(field, samples, gain, offset):
    width = field.shape[-1]
    grouped = field.reshape(samples, -1, GROUPS, width // GROUPS)
    center = jnp.mean(grouped, axis=(1, 3), keepdims=True)
    spread = jnp.mean((grouped - center) ** 2, axis=(1, 3), keepdims=True)
    normed = ((grouped - center) * lax.rsqrt(spread + 1e-05)).reshape(field.shape)
    return normed * gain + offset


def shifted(field, offset, valid, pad):
    padded = jnp.pad(field, ((pad, pad), (0, 0)))
    rows = field.shape[0]
    piece = padded[pad + offset : pad + offset + rows]
    return jnp.where(valid, piece, jnp.zeros_like(piece))


def spatial_conv(first, spatial3, frames, rows, cols):
    positions = first.shape[0]
    products = jnp.einsum(
        "pc,tco->tpo", first, spatial3, precision=precise, preferred_element_type=jnp.float32
    )
    pos = lax.broadcasted_iota(jnp.int32, (positions, 1), 0)
    within = pos % (rows * cols)
    row = within // cols
    col = within % cols
    total = None
    for delta_row in range(3):
        for delta_col in range(3):
            r = row + delta_row - 1
            c = col + delta_col - 1
            valid = (r >= 0) & (r < rows) & (c >= 0) & (c < cols)
            offset = (delta_row - 1) * cols + (delta_col - 1)
            piece = shifted(products[3 * delta_row + delta_col], offset, valid, cols + 1)
            total = piece if total is None else total + piece
    return total


def temporal_conv(second, temporal3, frames, rows, cols):
    positions = second.shape[0]
    plane = rows * cols
    products = jnp.einsum(
        "pc,tco->tpo", second, temporal3, precision=precise, preferred_element_type=jnp.float32
    )
    pos = lax.broadcasted_iota(jnp.int32, (positions, 1), 0)
    frame = (pos // plane) % frames
    total = None
    for tap in range(3):
        f = frame + tap - 1
        valid = (f >= 0) & (f < frames)
        piece = shifted(products[tap], (tap - 1) * plane, valid, plane)
        total = piece if total is None else total + piece
    return total


def section(x, skip_in, spatial3, temporal3, skip_mat, gains, offsets, dims):
    samples, frames, rows, cols = dims
    if skip_in is None:
        hidden = x
    else:
        hidden = x + jnp.dot(
            skip_in, skip_mat, precision=precise, preferred_element_type=jnp.float32
        )
    first = jax.nn.silu(group_norm(hidden, samples, gains[0], offsets[0]))
    mixed = hidden + spatial_conv(first, spatial3, frames, rows, cols)
    second = jax.nn.silu(group_norm(mixed, samples, gains[1], offsets[1]))
    return mixed + temporal_conv(second, temporal3, frames, rows, cols)


def per_device(latents, spatial_weight, temporal_weight, skip_weight, norm_gain, norm_bias):
    sections = lax.axis_size("segment")
    position = lax.axis_index("segment")
    steps_total = MICRO + sections - 1
    gains = norm_gain[0]
    offsets = norm_bias[0]
    width = spatial_weight.shape[-1]
    micro, samples, frames, rows, cols = latents.shape[:5]
    dims = (samples, frames, rows, cols)
    flat = latents.reshape(micro, -1, width)
    rs, rt = spatial_weight.shape[1], temporal_weight.shape[1]
    pack = jnp.concatenate([spatial_weight[0], temporal_weight[0], skip_weight[0]], axis=0)
    gathered = lax.all_gather(pack, "fsdp", axis=0, tiled=False)
    spatial3 = gathered[:, :rs].reshape(9, width, width)
    temporal3 = gathered[:, rs : rs + rt].reshape(3, width, width)
    skip_mat = gathered[:, rs + rt :].reshape(width, width)
    blank = jnp.zeros_like(flat[0])
    results = [blank] * MICRO
    skips = [None] * MICRO
    previous = blank
    for moment in range(steps_total):
        if moment == 0:
            incoming = blank
        else:
            pairs = [
                (s, s + 1) for s in range(sections - 1) if 0 <= moment - 1 - s < MICRO
            ]
            incoming = lax.ppermute(previous, "segment", pairs)
        fresh = flat[min(moment, MICRO - 1)] if moment < MICRO else blank
        stream = jnp.where(position == 0, fresh, incoming)
        late_index = moment - (sections - 1)
        skip_in = skips[late_index] if 0 <= late_index < MICRO else None
        output = section(stream, skip_in, spatial3, temporal3, skip_mat, gains, offsets, dims)
        which = moment - position
        for slot_index in range(MICRO):
            results[slot_index] = jnp.where(which == slot_index, output, results[slot_index])
        if moment < MICRO:
            skips[moment] = lax.ppermute(output, "segment", [(0, sections - 1)])
        previous = output
    return jnp.stack(results).reshape((1,) + latents.shape)


def solution(mesh):
    placed = (
        P(None, "fsdp", None, None, None, None),
        P("segment", "fsdp", None),
        P("segment", "fsdp", None),
        P("segment", "fsdp", None),
        P("segment", None, None),
        P("segment", None, None),
    )
    return jax.shard_map(
        per_device,
        mesh=mesh,
        in_specs=placed,
        out_specs=P("segment", None, "fsdp", None, None, None, None),
        check_vma=False,
    )
```

```python
import functools

import jax
import jax.numpy as jnp
from jax import lax
from jax.sharding import PartitionSpec as P

GROUPS = 32
MICRO = 2


precise = lax.Precision.HIGH


def group_norm(field, samples, gain, offset):
    width = field.shape[-1]
    grouped = field.reshape(samples, -1, GROUPS, width // GROUPS)
    center = jnp.mean(grouped, axis=(1, 3), keepdims=True)
    spread = jnp.mean((grouped - center) ** 2, axis=(1, 3), keepdims=True)
    normed = ((grouped - center) * lax.rsqrt(spread + 1e-05)).reshape(field.shape)
    return normed * gain + offset


def shifted(field, offset, valid, pad):
    padded = jnp.pad(field, ((pad, pad), (0, 0)))
    rows = field.shape[0]
    piece = padded[pad + offset : pad + offset + rows]
    return jnp.where(valid, piece, jnp.zeros_like(piece))


def spatial_conv(first, spatial3, frames, rows, cols):
    positions = first.shape[0]
    products = jnp.einsum(
        "pc,tco->tpo", first, spatial3, precision=precise, preferred_element_type=jnp.float32
    )
    pos = lax.broadcasted_iota(jnp.int32, (positions, 1), 0)
    within = pos % (rows * cols)
    row = within // cols
    col = within % cols
    total = None
    for delta_row in range(3):
        for delta_col in range(3):
            r = row + delta_row - 1
            c = col + delta_col - 1
            valid = (r >= 0) & (r < rows) & (c >= 0) & (c < cols)
            offset = (delta_row - 1) * cols + (delta_col - 1)
            piece = shifted(products[3 * delta_row + delta_col], offset, valid, cols + 1)
            total = piece if total is None else total + piece
    return total


def temporal_conv(second, temporal3, frames, rows, cols):
    positions = second.shape[0]
    plane = rows * cols
    products = jnp.einsum(
        "pc,tco->tpo", second, temporal3, precision=precise, preferred_element_type=jnp.float32
    )
    pos = lax.broadcasted_iota(jnp.int32, (positions, 1), 0)
    frame = (pos // plane) % frames
    total = None
    for tap in range(3):
        f = frame + tap - 1
        valid = (f >= 0) & (f < frames)
        piece = shifted(products[tap], (tap - 1) * plane, valid, plane)
        total = piece if total is None else total + piece
    return total


def section(x, skip_in, spatial3, temporal3, skip_mat, gains, offsets, dims):
    samples, frames, rows, cols = dims
    if skip_in is None:
        hidden = x
    else:
        hidden = x + jnp.dot(
            skip_in, skip_mat, precision=precise, preferred_element_type=jnp.float32
        )
    first = jax.nn.silu(group_norm(hidden, samples, gains[0], offsets[0]))
    mixed = hidden + spatial_conv(first, spatial3, frames, rows, cols)
    second = jax.nn.silu(group_norm(mixed, samples, gains[1], offsets[1]))
    return mixed + temporal_conv(second, temporal3, frames, rows, cols)


def ring_gather(pack, axis, ring):
    size = len(ring)
    place = [0] * size
    for spot, member in enumerate(ring):
        place[member] = spot
    me = lax.axis_index(axis)
    spot = jnp.array(place, jnp.int32)[me]
    members = jnp.array(ring, jnp.int32)
    out = jnp.zeros((size,) + pack.shape, pack.dtype)
    out = lax.dynamic_update_index_in_dim(out, pack, me, 0)
    ahead = [(ring[j], ring[(j + 1) % size]) for j in range(size)]
    behind = [(ring[(j + 1) % size], ring[j]) for j in range(size)]
    forward = backward = pack
    steps_forward = size // 2
    steps_backward = size - 1 - steps_forward
    for step in range(1, steps_forward + 1):
        forward = lax.ppermute(forward, axis, ahead)
        out = lax.dynamic_update_index_in_dim(out, forward, members[(spot - step) % size], 0)
        if step <= steps_backward:
            backward = lax.ppermute(backward, axis, behind)
            out = lax.dynamic_update_index_in_dim(
                out, backward, members[(spot + step) % size], 0
            )
    return out


def neighbour_ring(mesh, axis):
    names = list(mesh.axis_names)
    where = names.index(axis)
    grid = mesh.devices.transpose([i for i in range(len(names)) if i != where] + [where])
    rows = grid.reshape(-1, grid.shape[-1])
    size = rows.shape[1]
    if size < 3 or size > 16:
        return None

    def near(row, a, b):
        ca, cb = row[a].coords, row[b].coords
        return sum(abs(int(u) - int(v)) for u, v in zip(ca, cb)) == 1

    first = rows[0]
    path = [0]

    def extend():
        if len(path) == size:
            return near(first, path[-1], path[0])
        for nxt in range(size):
            if nxt not in path and near(first, path[-1], nxt):
                path.append(nxt)
                if extend():
                    return True
                path.pop()
        return False

    if not extend():
        return None
    for row in rows:
        if not all(near(row, path[j], path[(j + 1) % size]) for j in range(size)):
            return None
    return tuple(path)


def per_device(ring, latents, spatial_weight, temporal_weight, skip_weight, norm_gain, norm_bias):
    sections = lax.axis_size("segment")
    position = lax.axis_index("segment")
    steps_total = MICRO + sections - 1
    gains = norm_gain[0]
    offsets = norm_bias[0]
    width = spatial_weight.shape[-1]
    micro, samples, frames, rows, cols = latents.shape[:5]
    dims = (samples, frames, rows, cols)
    flat = latents.reshape(micro, -1, width)
    rs, rt = spatial_weight.shape[1], temporal_weight.shape[1]
    pack = jnp.concatenate([spatial_weight[0], temporal_weight[0], skip_weight[0]], axis=0)
    if ring is None:
        gathered = lax.all_gather(pack, "fsdp", axis=0, tiled=False)
    else:
        gathered = ring_gather(pack, "fsdp", ring)
    spatial3 = gathered[:, :rs].reshape(9, width, width)
    temporal3 = gathered[:, rs : rs + rt].reshape(3, width, width)
    skip_mat = gathered[:, rs + rt :].reshape(width, width)
    blank = jnp.zeros_like(flat[0])
    results = [blank] * MICRO
    skips = [None] * MICRO
    previous = blank
    for moment in range(steps_total):
        if moment == 0:
            incoming = blank
        else:
            pairs = [
                (s, s + 1) for s in range(sections - 1) if 0 <= moment - 1 - s < MICRO
            ]
            incoming = lax.ppermute(previous, "segment", pairs)
        fresh = flat[min(moment, MICRO - 1)] if moment < MICRO else blank
        stream = jnp.where(position == 0, fresh, incoming)
        late_index = moment - (sections - 1)
        skip_in = skips[late_index] if 0 <= late_index < MICRO else None
        output = section(stream, skip_in, spatial3, temporal3, skip_mat, gains, offsets, dims)
        which = moment - position
        for slot_index in range(MICRO):
            results[slot_index] = jnp.where(which == slot_index, output, results[slot_index])
        if moment < MICRO:
            skips[moment] = lax.ppermute(output, "segment", [(0, sections - 1)])
        previous = output
    return jnp.stack(results).reshape((1,) + latents.shape)


def solution(mesh):
    placed = (
        P(None, "fsdp", None, None, None, None),
        P("segment", "fsdp", None),
        P("segment", "fsdp", None),
        P("segment", "fsdp", None),
        P("segment", None, None),
        P("segment", None, None),
    )
    ring = neighbour_ring(mesh, "fsdp")
    return jax.shard_map(
        functools.partial(per_device, ring),
        mesh=mesh,
        in_specs=placed,
        out_specs=P("segment", None, "fsdp", None, None, None, None),
        check_vma=False,
    )
```

```python
import functools

import jax
import jax.numpy as jnp
from jax import lax
from jax.sharding import PartitionSpec as P

GROUPS = 32
MICRO = 2


precise = lax.Precision.HIGH


def group_norm(field, samples, gain, offset):
    width = field.shape[-1]
    grouped = field.reshape(samples, -1, GROUPS, width // GROUPS)
    center = jnp.mean(grouped, axis=(1, 3), keepdims=True)
    spread = jnp.mean((grouped - center) ** 2, axis=(1, 3), keepdims=True)
    normed = ((grouped - center) * lax.rsqrt(spread + 1e-05)).reshape(field.shape)
    return normed * gain + offset


def shifted(field, offset, valid, pad):
    padded = jnp.pad(field, ((pad, pad), (0, 0)))
    rows = field.shape[0]
    piece = padded[pad + offset : pad + offset + rows]
    return jnp.where(valid, piece, jnp.zeros_like(piece))


def spatial_conv(first, spatial3, frames, rows, cols):
    positions = first.shape[0]
    products = jnp.einsum(
        "pc,tco->tpo", first, spatial3, precision=precise, preferred_element_type=jnp.float32
    )
    pos = lax.broadcasted_iota(jnp.int32, (positions, 1), 0)
    within = pos % (rows * cols)
    row = within // cols
    col = within % cols
    total = None
    for delta_row in range(3):
        for delta_col in range(3):
            r = row + delta_row - 1
            c = col + delta_col - 1
            valid = (r >= 0) & (r < rows) & (c >= 0) & (c < cols)
            offset = (delta_row - 1) * cols + (delta_col - 1)
            piece = shifted(products[3 * delta_row + delta_col], offset, valid, cols + 1)
            total = piece if total is None else total + piece
    return total


def temporal_conv(second, temporal3, frames, rows, cols):
    positions = second.shape[0]
    plane = rows * cols
    products = jnp.einsum(
        "pc,tco->tpo", second, temporal3, precision=precise, preferred_element_type=jnp.float32
    )
    pos = lax.broadcasted_iota(jnp.int32, (positions, 1), 0)
    frame = (pos // plane) % frames
    total = None
    for tap in range(3):
        f = frame + tap - 1
        valid = (f >= 0) & (f < frames)
        piece = shifted(products[tap], (tap - 1) * plane, valid, plane)
        total = piece if total is None else total + piece
    return total


def section(x, skip_in, spatial3, temporal3, skip_mat, gains, offsets, dims):
    samples, frames, rows, cols = dims
    if skip_in is None:
        hidden = x
    else:
        hidden = x + jnp.dot(
            skip_in, skip_mat, precision=precise, preferred_element_type=jnp.float32
        )
    first = jax.nn.silu(group_norm(hidden, samples, gains[0], offsets[0]))
    mixed = hidden + spatial_conv(first, spatial3, frames, rows, cols)
    second = jax.nn.silu(group_norm(mixed, samples, gains[1], offsets[1]))
    return mixed + temporal_conv(second, temporal3, frames, rows, cols)


def ring_gather(pack, axis, ring):
    size = len(ring)
    place = [0] * size
    for spot, member in enumerate(ring):
        place[member] = spot
    me = lax.axis_index(axis)
    spot = jnp.array(place, jnp.int32)[me]
    members = jnp.array(ring, jnp.int32)
    out = jnp.zeros((size,) + pack.shape, pack.dtype)
    out = lax.dynamic_update_index_in_dim(out, pack, me, 0)
    ahead = [(ring[j], ring[(j + 1) % size]) for j in range(size)]
    behind = [(ring[(j + 1) % size], ring[j]) for j in range(size)]
    forward = backward = pack
    steps_forward = size // 2
    steps_backward = size - 1 - steps_forward
    for step in range(1, steps_forward + 1):
        forward = lax.ppermute(forward, axis, ahead)
        out = lax.dynamic_update_index_in_dim(out, forward, members[(spot - step) % size], 0)
        if step <= steps_backward:
            backward = lax.ppermute(backward, axis, behind)
            out = lax.dynamic_update_index_in_dim(
                out, backward, members[(spot + step) % size], 0
            )
    return out, forward


def neighbour_ring(mesh, axis):
    names = list(mesh.axis_names)
    where = names.index(axis)
    grid = mesh.devices.transpose([i for i in range(len(names)) if i != where] + [where])
    rows = grid.reshape(-1, grid.shape[-1])
    size = rows.shape[1]
    if size < 3 or size > 16:
        return None

    def near(row, a, b):
        ca, cb = row[a].coords, row[b].coords
        return sum(abs(int(u) - int(v)) for u, v in zip(ca, cb)) == 1

    first = rows[0]
    path = [0]

    def extend():
        if len(path) == size:
            return near(first, path[-1], path[0])
        for nxt in range(size):
            if nxt not in path and near(first, path[-1], nxt):
                path.append(nxt)
                if extend():
                    return True
                path.pop()
        return False

    if not extend():
        return None
    for row in rows:
        if not all(near(row, path[j], path[(j + 1) % size]) for j in range(size)):
            return None
    return tuple(path)


def per_device(ring, latents, spatial_weight, temporal_weight, skip_weight, norm_gain, norm_bias):
    sections = lax.axis_size("segment")
    position = lax.axis_index("segment")
    steps_total = MICRO + sections - 1
    gains = norm_gain[0]
    offsets = norm_bias[0]
    width = spatial_weight.shape[-1]
    micro, samples, frames, rows, cols = latents.shape[:5]
    dims = (samples, frames, rows, cols)
    flat = latents.reshape(micro, -1, width)
    if ring is None:
        spatial_all = lax.all_gather(spatial_weight[0], "fsdp", axis=0, tiled=True)
        temporal_all = lax.all_gather(temporal_weight[0], "fsdp", axis=0, tiled=True)
        skip_all = lax.all_gather(skip_weight[0], "fsdp", axis=0, tiled=True)
    else:
        spatial_all, last = ring_gather(spatial_weight[0], "fsdp", ring)
        temporal_in, _ = lax.optimization_barrier((temporal_weight[0], last))
        temporal_all, last = ring_gather(temporal_in, "fsdp", ring)
        skip_in, _ = lax.optimization_barrier((skip_weight[0], last))
        skip_all = lax.all_gather(skip_in, "fsdp", axis=0, tiled=True)
    spatial3 = spatial_all.reshape(9, width, width)
    temporal3 = temporal_all.reshape(3, width, width)
    skip_mat = skip_all.reshape(width, width)
    blank = jnp.zeros_like(flat[0])
    results = [blank] * MICRO
    skips = [None] * MICRO
    previous = blank
    for moment in range(steps_total):
        if moment == 0:
            incoming = blank
        else:
            pairs = [
                (s, s + 1) for s in range(sections - 1) if 0 <= moment - 1 - s < MICRO
            ]
            incoming = lax.ppermute(previous, "segment", pairs)
        fresh = flat[min(moment, MICRO - 1)] if moment < MICRO else blank
        stream = jnp.where(position == 0, fresh, incoming)
        late_index = moment - (sections - 1)
        skip_in = skips[late_index] if 0 <= late_index < MICRO else None
        output = section(stream, skip_in, spatial3, temporal3, skip_mat, gains, offsets, dims)
        which = moment - position
        for slot_index in range(MICRO):
            results[slot_index] = jnp.where(which == slot_index, output, results[slot_index])
        if moment < MICRO:
            skips[moment] = lax.ppermute(output, "segment", [(0, sections - 1)])
        previous = output
    return jnp.stack(results).reshape((1,) + latents.shape)


def solution(mesh):
    placed = (
        P(None, "fsdp", None, None, None, None),
        P("segment", "fsdp", None),
        P("segment", "fsdp", None),
        P("segment", "fsdp", None),
        P("segment", None, None),
        P("segment", None, None),
    )
    ring = neighbour_ring(mesh, "fsdp")
    return jax.shard_map(
        functools.partial(per_device, ring),
        mesh=mesh,
        in_specs=placed,
        out_specs=P("segment", None, "fsdp", None, None, None, None),
        check_vma=False,
    )
```

```python
import functools

import jax
import jax.numpy as jnp
from jax import lax
from jax.sharding import PartitionSpec as P

GROUPS = 32
MICRO = 2


precise = lax.Precision.HIGH


def group_norm(field, samples, gain, offset):
    width = field.shape[-1]
    grouped = field.reshape(samples, -1, GROUPS, width // GROUPS)
    center = jnp.mean(grouped, axis=(1, 3), keepdims=True)
    spread = jnp.mean((grouped - center) ** 2, axis=(1, 3), keepdims=True)
    normed = ((grouped - center) * lax.rsqrt(spread + 1e-05)).reshape(field.shape)
    return normed * gain + offset


def shifted(field, offset, valid, pad):
    padded = jnp.pad(field, ((pad, pad), (0, 0)))
    rows = field.shape[0]
    piece = padded[pad + offset : pad + offset + rows]
    return jnp.where(valid, piece, jnp.zeros_like(piece))


def spatial_conv(first, spatial3, frames, rows, cols):
    positions = first.shape[0]
    products = jnp.einsum(
        "pc,tco->tpo", first, spatial3, precision=precise, preferred_element_type=jnp.float32
    )
    pos = lax.broadcasted_iota(jnp.int32, (positions, 1), 0)
    within = pos % (rows * cols)
    row = within // cols
    col = within % cols
    total = None
    for delta_row in range(3):
        for delta_col in range(3):
            r = row + delta_row - 1
            c = col + delta_col - 1
            valid = (r >= 0) & (r < rows) & (c >= 0) & (c < cols)
            offset = (delta_row - 1) * cols + (delta_col - 1)
            piece = shifted(products[3 * delta_row + delta_col], offset, valid, cols + 1)
            total = piece if total is None else total + piece
    return total


def temporal_conv(second, temporal3, frames, rows, cols):
    positions = second.shape[0]
    plane = rows * cols
    products = jnp.einsum(
        "pc,tco->tpo", second, temporal3, precision=precise, preferred_element_type=jnp.float32
    )
    pos = lax.broadcasted_iota(jnp.int32, (positions, 1), 0)
    frame = (pos // plane) % frames
    total = None
    for tap in range(3):
        f = frame + tap - 1
        valid = (f >= 0) & (f < frames)
        piece = shifted(products[tap], (tap - 1) * plane, valid, plane)
        total = piece if total is None else total + piece
    return total


def section(x, skip_in, spatial3, temporal3, skip_mat, gains, offsets, dims):
    samples, frames, rows, cols = dims
    if skip_in is None:
        hidden = x
    else:
        hidden = x + jnp.dot(
            skip_in, skip_mat, precision=precise, preferred_element_type=jnp.float32
        )
    first = jax.nn.silu(group_norm(hidden, samples, gains[0], offsets[0]))
    mixed = hidden + spatial_conv(first, spatial3, frames, rows, cols)
    second = jax.nn.silu(group_norm(mixed, samples, gains[1], offsets[1]))
    return mixed + temporal_conv(second, temporal3, frames, rows, cols)


def ring_gather(pack, axis, ring):
    size = len(ring)
    place = [0] * size
    for spot, member in enumerate(ring):
        place[member] = spot
    me = lax.axis_index(axis)
    spot = jnp.array(place, jnp.int32)[me]
    members = jnp.array(ring, jnp.int32)
    out = jnp.zeros((size,) + pack.shape, pack.dtype)
    out = lax.dynamic_update_index_in_dim(out, pack, me, 0)
    ahead = [(ring[j], ring[(j + 1) % size]) for j in range(size)]
    behind = [(ring[(j + 1) % size], ring[j]) for j in range(size)]
    forward = backward = pack
    steps_forward = size // 2
    steps_backward = size - 1 - steps_forward
    for step in range(1, steps_forward + 1):
        forward = lax.ppermute(forward, axis, ahead)
        out = lax.dynamic_update_index_in_dim(out, forward, members[(spot - step) % size], 0)
        if step <= steps_backward:
            backward = lax.ppermute(backward, axis, behind)
            out = lax.dynamic_update_index_in_dim(
                out, backward, members[(spot + step) % size], 0
            )
    return out


def neighbour_ring(mesh, axis):
    names = list(mesh.axis_names)
    where = names.index(axis)
    grid = mesh.devices.transpose([i for i in range(len(names)) if i != where] + [where])
    rows = grid.reshape(-1, grid.shape[-1])
    size = rows.shape[1]
    if size < 3 or size > 16:
        return None

    def near(row, a, b):
        ca, cb = row[a].coords, row[b].coords
        return sum(abs(int(u) - int(v)) for u, v in zip(ca, cb)) == 1

    first = rows[0]
    path = [0]

    def extend():
        if len(path) == size:
            return near(first, path[-1], path[0])
        for nxt in range(size):
            if nxt not in path and near(first, path[-1], nxt):
                path.append(nxt)
                if extend():
                    return True
                path.pop()
        return False

    if not extend():
        return None
    for row in rows:
        if not all(near(row, path[j], path[(j + 1) % size]) for j in range(size)):
            return None
    return tuple(path)


def per_device(ring, latents, spatial_weight, temporal_weight, skip_weight, norm_gain, norm_bias):
    sections = lax.axis_size("segment")
    position = lax.axis_index("segment")
    steps_total = MICRO + sections - 1
    gains = norm_gain[0]
    offsets = norm_bias[0]
    width = spatial_weight.shape[-1]
    micro, samples, frames, rows, cols = latents.shape[:5]
    dims = (samples, frames, rows, cols)
    flat = latents.reshape(micro, -1, width)
    rs, rt, rk = spatial_weight.shape[1], temporal_weight.shape[1], skip_weight.shape[1]
    if ring is None:
        pack = jnp.concatenate([spatial_weight[0], temporal_weight[0]], axis=0)
        gathered = lax.all_gather(pack, "fsdp", axis=0, tiled=False)
    else:
        pack = jnp.concatenate([spatial_weight[0], temporal_weight[0]], axis=0)
        gathered = ring_gather(pack, "fsdp", ring)
    spatial3 = gathered[:, :rs].reshape(9, width, width)
    temporal3 = gathered[:, rs : rs + rt].reshape(3, width, width)
    blank = jnp.zeros_like(flat[0])
    results = [blank] * MICRO
    skips = [None] * MICRO
    skip_mat = None
    previous = blank
    for moment in range(steps_total):
        if moment == 0:
            stream = flat[0]
        else:
            pairs = [
                (s, s + 1) for s in range(sections - 1) if 0 <= moment - 1 - s < MICRO
            ]
            incoming = lax.ppermute(previous, "segment", pairs)
            if moment < MICRO:
                stream = jnp.where(position == 0, flat[moment], incoming)
            else:
                stream = incoming
        late_index = moment - (sections - 1)
        skip_in = skips[late_index] if 0 <= late_index < MICRO else None
        output = section(stream, skip_in, spatial3, temporal3, skip_mat, gains, offsets, dims)
        which = moment - position
        for slot_index in range(MICRO):
            results[slot_index] = jnp.where(which == slot_index, output, results[slot_index])
        if moment < MICRO:
            skips[moment] = lax.ppermute(output, "segment", [(0, sections - 1)])
        if moment == 0:
            shard, _ = lax.optimization_barrier((skip_weight[0], output))
            spare = max(0, 3 * rk - shard.shape[0])
            padded = jnp.pad(shard, ((0, spare), (0, 0)))
            skip_all = lax.all_gather(padded, "fsdp", axis=0, tiled=False)
            skip_mat = skip_all[:, :rk].reshape(width, width)
        previous = output
    return jnp.stack(results).reshape((1,) + latents.shape)


def solution(mesh):
    placed = (
        P(None, "fsdp", None, None, None, None),
        P("segment", "fsdp", None),
        P("segment", "fsdp", None),
        P("segment", "fsdp", None),
        P("segment", None, None),
        P("segment", None, None),
    )
    ring = neighbour_ring(mesh, "fsdp")
    return jax.shard_map(
        functools.partial(per_device, ring),
        mesh=mesh,
        in_specs=placed,
        out_specs=P("segment", None, "fsdp", None, None, None, None),
        check_vma=False,
    )
```

```python
import functools

import jax
import jax.numpy as jnp
from jax import lax
from jax.sharding import PartitionSpec as P

GROUPS = 32
MICRO = 2


precise = lax.Precision.HIGH


def group_norm(field, samples, gain, offset):
    width = field.shape[-1]
    grouped = field.reshape(samples, -1, GROUPS, width // GROUPS)
    center = jnp.mean(grouped, axis=(1, 3), keepdims=True)
    spread = jnp.mean((grouped - center) ** 2, axis=(1, 3), keepdims=True)
    normed = ((grouped - center) * lax.rsqrt(spread + 1e-05)).reshape(field.shape)
    return normed * gain + offset


def shifted(field, offset, valid, pad):
    padded = jnp.pad(field, ((pad, pad), (0, 0)))
    rows = field.shape[0]
    piece = padded[pad + offset : pad + offset + rows]
    return jnp.where(valid, piece, jnp.zeros_like(piece))


def spatial_conv(first, spatial3, frames, rows, cols):
    positions = first.shape[0]
    products = jnp.einsum(
        "pc,tco->tpo", first, spatial3, precision=precise, preferred_element_type=jnp.float32
    )
    pos = lax.broadcasted_iota(jnp.int32, (positions, 1), 0)
    within = pos % (rows * cols)
    row = within // cols
    col = within % cols
    total = None
    for delta_row in range(3):
        for delta_col in range(3):
            r = row + delta_row - 1
            c = col + delta_col - 1
            valid = (r >= 0) & (r < rows) & (c >= 0) & (c < cols)
            offset = (delta_row - 1) * cols + (delta_col - 1)
            piece = shifted(products[3 * delta_row + delta_col], offset, valid, cols + 1)
            total = piece if total is None else total + piece
    return total


def temporal_conv(second, temporal3, frames, rows, cols):
    positions = second.shape[0]
    plane = rows * cols
    products = jnp.einsum(
        "pc,tco->tpo", second, temporal3, precision=precise, preferred_element_type=jnp.float32
    )
    pos = lax.broadcasted_iota(jnp.int32, (positions, 1), 0)
    frame = (pos // plane) % frames
    total = None
    for tap in range(3):
        f = frame + tap - 1
        valid = (f >= 0) & (f < frames)
        piece = shifted(products[tap], (tap - 1) * plane, valid, plane)
        total = piece if total is None else total + piece
    return total


def prepare(x, skip_in, skip_mat, gains, offsets, dims):
    samples = dims[0]
    if skip_in is None:
        hidden = x
    else:
        hidden = x + jnp.dot(
            skip_in, skip_mat, precision=precise, preferred_element_type=jnp.float32
        )
    first = jax.nn.silu(group_norm(hidden, samples, gains[0], offsets[0]))
    return hidden, first


def finish(hidden, first, spatial3, temporal3, gains, offsets, dims):
    samples, frames, rows, cols = dims
    mixed = hidden + spatial_conv(first, spatial3, frames, rows, cols)
    second = jax.nn.silu(group_norm(mixed, samples, gains[1], offsets[1]))
    return mixed + temporal_conv(second, temporal3, frames, rows, cols)


def ring_gather(pack, axis, ring):
    size = len(ring)
    place = [0] * size
    for spot, member in enumerate(ring):
        place[member] = spot
    me = lax.axis_index(axis)
    spot = jnp.array(place, jnp.int32)[me]
    members = jnp.array(ring, jnp.int32)
    out = jnp.zeros((size,) + pack.shape, pack.dtype)
    out = lax.dynamic_update_index_in_dim(out, pack, me, 0)
    ahead = [(ring[j], ring[(j + 1) % size]) for j in range(size)]
    behind = [(ring[(j + 1) % size], ring[j]) for j in range(size)]
    forward = backward = pack
    steps_forward = size // 2
    steps_backward = size - 1 - steps_forward
    for step in range(1, steps_forward + 1):
        forward = lax.ppermute(forward, axis, ahead)
        out = lax.dynamic_update_index_in_dim(out, forward, members[(spot - step) % size], 0)
        if step <= steps_backward:
            backward = lax.ppermute(backward, axis, behind)
            out = lax.dynamic_update_index_in_dim(
                out, backward, members[(spot + step) % size], 0
            )
    return out, forward


def neighbour_ring(mesh, axis):
    names = list(mesh.axis_names)
    where = names.index(axis)
    grid = mesh.devices.transpose([i for i in range(len(names)) if i != where] + [where])
    rows = grid.reshape(-1, grid.shape[-1])
    size = rows.shape[1]
    if size < 3 or size > 16:
        return None

    def near(row, a, b):
        ca, cb = row[a].coords, row[b].coords
        return sum(abs(int(u) - int(v)) for u, v in zip(ca, cb)) == 1

    first = rows[0]
    path = [0]

    def extend():
        if len(path) == size:
            return near(first, path[-1], path[0])
        for nxt in range(size):
            if nxt not in path and near(first, path[-1], nxt):
                path.append(nxt)
                if extend():
                    return True
                path.pop()
        return False

    if not extend():
        return None
    for row in rows:
        if not all(near(row, path[j], path[(j + 1) % size]) for j in range(size)):
            return None
    return tuple(path)


def per_device(ring, latents, spatial_weight, temporal_weight, skip_weight, norm_gain, norm_bias):
    sections = lax.axis_size("segment")
    position = lax.axis_index("segment")
    steps_total = MICRO + sections - 1
    gains = norm_gain[0]
    offsets = norm_bias[0]
    width = spatial_weight.shape[-1]
    micro, samples, frames, rows, cols = latents.shape[:5]
    dims = (samples, frames, rows, cols)
    flat = latents.reshape(micro, -1, width)
    rt = temporal_weight.shape[1]
    hidden0, first0 = prepare(flat[0], None, None, gains, offsets, dims)
    pack = jnp.concatenate([temporal_weight[0], skip_weight[0]], axis=0)
    if ring is None:
        spatial_all = lax.all_gather(spatial_weight[0], "fsdp", axis=0, tiled=True)
        rest = lax.all_gather(pack, "fsdp", axis=0, tiled=False)
    else:
        spatial_in, _ = lax.optimization_barrier((spatial_weight[0], first0))
        spatial_all, last = ring_gather(spatial_in, "fsdp", ring)
        rest_in, _ = lax.optimization_barrier((pack, last))
        rest, _ = ring_gather(rest_in, "fsdp", ring)
    spatial3 = spatial_all.reshape(9, width, width)
    temporal3 = rest[:, :rt].reshape(3, width, width)
    skip_mat = rest[:, rt:].reshape(width, width)
    blank = jnp.zeros_like(flat[0])
    results = [blank] * MICRO
    skips = [None] * MICRO
    previous = blank
    for moment in range(steps_total):
        if moment == 0:
            hidden, first = hidden0, first0
        else:
            pairs = [
                (s, s + 1) for s in range(sections - 1) if 0 <= moment - 1 - s < MICRO
            ]
            incoming = lax.ppermute(previous, "segment", pairs)
            if moment < MICRO:
                stream = jnp.where(position == 0, flat[moment], incoming)
            else:
                stream = incoming
            late_index = moment - (sections - 1)
            skip_in = skips[late_index] if 0 <= late_index < MICRO else None
            hidden, first = prepare(stream, skip_in, skip_mat, gains, offsets, dims)
        output = finish(hidden, first, spatial3, temporal3, gains, offsets, dims)
        which = moment - position
        for slot_index in range(MICRO):
            results[slot_index] = jnp.where(which == slot_index, output, results[slot_index])
        if moment < MICRO:
            skips[moment] = lax.ppermute(output, "segment", [(0, sections - 1)])
        previous = output
    return jnp.stack(results).reshape((1,) + latents.shape)


def solution(mesh):
    placed = (
        P(None, "fsdp", None, None, None, None),
        P("segment", "fsdp", None),
        P("segment", "fsdp", None),
        P("segment", "fsdp", None),
        P("segment", None, None),
        P("segment", None, None),
    )
    ring = neighbour_ring(mesh, "fsdp")
    return jax.shard_map(
        functools.partial(per_device, ring),
        mesh=mesh,
        in_specs=placed,
        out_specs=P("segment", None, "fsdp", None, None, None, None),
        check_vma=False,
    )
```

```python
import functools

import jax
import jax.numpy as jnp
from jax import lax
from jax.sharding import PartitionSpec as P

GROUPS = 32
MICRO = 2


precise = lax.Precision.HIGH


def group_norm(field, samples, gain, offset):
    width = field.shape[-1]
    grouped = field.reshape(samples, -1, GROUPS, width // GROUPS)
    center = jnp.mean(grouped, axis=(1, 3), keepdims=True)
    spread = jnp.mean((grouped - center) ** 2, axis=(1, 3), keepdims=True)
    normed = ((grouped - center) * lax.rsqrt(spread + 1e-05)).reshape(field.shape)
    return normed * gain + offset


def shifted(field, offset, valid, pad):
    padded = jnp.pad(field, ((pad, pad), (0, 0)))
    rows = field.shape[0]
    piece = padded[pad + offset : pad + offset + rows]
    return jnp.where(valid, piece, jnp.zeros_like(piece))


def spatial_conv(first, spatial3, frames, rows, cols):
    positions = first.shape[0]
    products = jnp.einsum(
        "pc,tco->tpo", first, spatial3, precision=precise, preferred_element_type=jnp.float32
    )
    pos = lax.broadcasted_iota(jnp.int32, (positions, 1), 0)
    within = pos % (rows * cols)
    row = within // cols
    col = within % cols
    total = None
    for delta_row in range(3):
        for delta_col in range(3):
            r = row + delta_row - 1
            c = col + delta_col - 1
            valid = (r >= 0) & (r < rows) & (c >= 0) & (c < cols)
            offset = (delta_row - 1) * cols + (delta_col - 1)
            piece = shifted(products[3 * delta_row + delta_col], offset, valid, cols + 1)
            total = piece if total is None else total + piece
    return total


def temporal_conv(second, temporal3, frames, rows, cols):
    positions = second.shape[0]
    plane = rows * cols
    products = jnp.einsum(
        "pc,tco->tpo", second, temporal3, precision=precise, preferred_element_type=jnp.float32
    )
    pos = lax.broadcasted_iota(jnp.int32, (positions, 1), 0)
    frame = (pos // plane) % frames
    total = None
    for tap in range(3):
        f = frame + tap - 1
        valid = (f >= 0) & (f < frames)
        piece = shifted(products[tap], (tap - 1) * plane, valid, plane)
        total = piece if total is None else total + piece
    return total


def section(x, skip_in, spatial3, temporal3, skip_mat, gains, offsets, dims):
    samples, frames, rows, cols = dims
    if skip_in is None:
        hidden = x
    else:
        hidden = x + jnp.dot(
            skip_in, skip_mat, precision=precise, preferred_element_type=jnp.float32
        )
    first = jax.nn.silu(group_norm(hidden, samples, gains[0], offsets[0]))
    mixed = hidden + spatial_conv(first, spatial3, frames, rows, cols)
    second = jax.nn.silu(group_norm(mixed, samples, gains[1], offsets[1]))
    return mixed + temporal_conv(second, temporal3, frames, rows, cols)


def ring_gather(pack, axis, ring):
    size = len(ring)
    place = [0] * size
    for spot, member in enumerate(ring):
        place[member] = spot
    me = lax.axis_index(axis)
    spot = jnp.array(place, jnp.int32)[me]
    members = jnp.array(ring, jnp.int32)
    out = jnp.zeros((size,) + pack.shape, pack.dtype)
    out = lax.dynamic_update_index_in_dim(out, pack, me, 0)
    ahead = [(ring[j], ring[(j + 1) % size]) for j in range(size)]
    behind = [(ring[(j + 1) % size], ring[j]) for j in range(size)]
    forward = backward = pack
    steps_forward = size // 2
    steps_backward = size - 1 - steps_forward
    for step in range(1, steps_forward + 1):
        forward = lax.ppermute(forward, axis, ahead)
        out = lax.dynamic_update_index_in_dim(out, forward, members[(spot - step) % size], 0)
        if step <= steps_backward:
            backward = lax.ppermute(backward, axis, behind)
            out = lax.dynamic_update_index_in_dim(
                out, backward, members[(spot + step) % size], 0
            )
    return out


def neighbour_ring(mesh, axis):
    names = list(mesh.axis_names)
    where = names.index(axis)
    grid = mesh.devices.transpose([i for i in range(len(names)) if i != where] + [where])
    rows = grid.reshape(-1, grid.shape[-1])
    size = rows.shape[1]
    if size < 3 or size > 16:
        return None

    def near(row, a, b):
        ca, cb = row[a].coords, row[b].coords
        return sum(abs(int(u) - int(v)) for u, v in zip(ca, cb)) == 1

    first = rows[0]
    path = [0]

    def extend():
        if len(path) == size:
            return near(first, path[-1], path[0])
        for nxt in range(size):
            if nxt not in path and near(first, path[-1], nxt):
                path.append(nxt)
                if extend():
                    return True
                path.pop()
        return False

    if not extend():
        return None
    for row in rows:
        if not all(near(row, path[j], path[(j + 1) % size]) for j in range(size)):
            return None
    return tuple(path)


def per_device(ring, latents, spatial_weight, temporal_weight, skip_weight, norm_gain, norm_bias):
    sections = lax.axis_size("segment")
    position = lax.axis_index("segment")
    steps_total = MICRO + sections - 1
    gains = norm_gain[0]
    offsets = norm_bias[0]
    width = spatial_weight.shape[-1]
    micro, samples, frames, rows, cols = latents.shape[:5]
    dims = (samples, frames, rows, cols)
    flat = latents.reshape(micro, -1, width)
    rs, rt = spatial_weight.shape[1], temporal_weight.shape[1]
    pack = jnp.concatenate([spatial_weight[0], temporal_weight[0], skip_weight[0]], axis=0)
    if ring is None:
        gathered = lax.all_gather(pack, "fsdp", axis=0, tiled=False)
    else:
        gathered = ring_gather(pack, "fsdp", ring)
    spatial3 = gathered[:, :rs].reshape(9, width, width)
    temporal3 = gathered[:, rs : rs + rt].reshape(3, width, width)
    skip_mat = gathered[:, rs + rt :].reshape(width, width)
    blank = jnp.zeros_like(flat[0])
    results = [blank] * MICRO
    skips = [None] * MICRO
    previous = blank
    for moment in range(steps_total):
        if moment == 0:
            stream = flat[0]
        else:
            pairs = [
                (s, s + 1) for s in range(sections - 1) if 0 <= moment - 1 - s < MICRO
            ]
            incoming = lax.ppermute(previous, "segment", pairs)
            if moment < MICRO:
                stream = jnp.where(position == 0, flat[moment], incoming)
            else:
                stream = incoming
        late_index = moment - (sections - 1)
        skip_in = skips[late_index] if 0 <= late_index < MICRO else None
        output = section(stream, skip_in, spatial3, temporal3, skip_mat, gains, offsets, dims)
        which = moment - position
        for slot_index in range(MICRO):
            results[slot_index] = jnp.where(which == slot_index, output, results[slot_index])
        if moment < MICRO:
            skips[moment] = lax.ppermute(output, "segment", [(0, sections - 1)])
        previous = output
    return jnp.stack(results).reshape((1,) + latents.shape)


def solution(mesh):
    placed = (
        P(None, "fsdp", None, None, None, None),
        P("segment", "fsdp", None),
        P("segment", "fsdp", None),
        P("segment", "fsdp", None),
        P("segment", None, None),
        P("segment", None, None),
    )
    ring = neighbour_ring(mesh, "fsdp")
    return jax.shard_map(
        functools.partial(per_device, ring),
        mesh=mesh,
        in_specs=placed,
        out_specs=P("segment", None, "fsdp", None, None, None, None),
        check_vma=False,
    )
```

```python
import functools

import jax
import jax.numpy as jnp
from jax import lax
from jax.sharding import PartitionSpec as P

GROUPS = 32
MICRO = 2


precise = lax.Precision.HIGH


def group_norm(field, samples, gain, offset):
    width = field.shape[-1]
    grouped = field.reshape(samples, -1, GROUPS, width // GROUPS)
    center = jnp.mean(grouped, axis=(1, 3), keepdims=True)
    spread = jnp.mean((grouped - center) ** 2, axis=(1, 3), keepdims=True)
    normed = ((grouped - center) * lax.rsqrt(spread + 1e-05)).reshape(field.shape)
    return normed * gain + offset


def shifted(field, offset, valid, pad):
    padded = jnp.pad(field, ((pad, pad), (0, 0)))
    rows = field.shape[0]
    piece = padded[pad + offset : pad + offset + rows]
    return jnp.where(valid, piece, jnp.zeros_like(piece))


def spatial_conv(first, spatial3, frames, rows, cols):
    positions = first.shape[0]
    products = jnp.einsum(
        "pc,tco->tpo", first, spatial3, precision=precise, preferred_element_type=jnp.float32
    )
    pos = lax.broadcasted_iota(jnp.int32, (positions, 1), 0)
    within = pos % (rows * cols)
    row = within // cols
    col = within % cols
    total = None
    for delta_row in range(3):
        for delta_col in range(3):
            r = row + delta_row - 1
            c = col + delta_col - 1
            valid = (r >= 0) & (r < rows) & (c >= 0) & (c < cols)
            offset = (delta_row - 1) * cols + (delta_col - 1)
            piece = shifted(products[3 * delta_row + delta_col], offset, valid, cols + 1)
            total = piece if total is None else total + piece
    return total


def temporal_conv(second, temporal3, frames, rows, cols):
    positions = second.shape[0]
    plane = rows * cols
    products = jnp.einsum(
        "pc,tco->tpo", second, temporal3, precision=precise, preferred_element_type=jnp.float32
    )
    pos = lax.broadcasted_iota(jnp.int32, (positions, 1), 0)
    frame = (pos // plane) % frames
    total = None
    for tap in range(3):
        f = frame + tap - 1
        valid = (f >= 0) & (f < frames)
        piece = shifted(products[tap], (tap - 1) * plane, valid, plane)
        total = piece if total is None else total + piece
    return total


def section(x, skip_in, spatial3, temporal3, skip_mat, gains, offsets, dims):
    samples, frames, rows, cols = dims
    if skip_in is None:
        hidden = x
    else:
        hidden = x + jnp.dot(
            skip_in, skip_mat, precision=precise, preferred_element_type=jnp.float32
        )
    first = jax.nn.silu(group_norm(hidden, samples, gains[0], offsets[0]))
    mixed = hidden + spatial_conv(first, spatial3, frames, rows, cols)
    second = jax.nn.silu(group_norm(mixed, samples, gains[1], offsets[1]))
    return mixed + temporal_conv(second, temporal3, frames, rows, cols)


def ring_gather(pack, axis, ring):
    size = len(ring)
    place = [0] * size
    for spot, member in enumerate(ring):
        place[member] = spot
    me = lax.axis_index(axis)
    spot = jnp.array(place, jnp.int32)[me]
    members = jnp.array(ring, jnp.int32)
    out = jnp.zeros((size,) + pack.shape, pack.dtype)
    out = lax.dynamic_update_index_in_dim(out, pack, me, 0)
    ahead = [(ring[j], ring[(j + 1) % size]) for j in range(size)]
    behind = [(ring[(j + 1) % size], ring[j]) for j in range(size)]
    forward = backward = pack
    steps_forward = size // 2
    steps_backward = size - 1 - steps_forward
    for step in range(1, steps_forward + 1):
        forward = lax.ppermute(forward, axis, ahead)
        out = lax.dynamic_update_index_in_dim(out, forward, members[(spot - step) % size], 0)
        if step <= steps_backward:
            backward = lax.ppermute(backward, axis, behind)
            out = lax.dynamic_update_index_in_dim(
                out, backward, members[(spot + step) % size], 0
            )
    return out


def neighbour_ring(mesh, axis):
    names = list(mesh.axis_names)
    where = names.index(axis)
    grid = mesh.devices.transpose([i for i in range(len(names)) if i != where] + [where])
    rows = grid.reshape(-1, grid.shape[-1])
    size = rows.shape[1]
    if size < 3 or size > 16:
        return None

    def near(row, a, b):
        ca, cb = row[a].coords, row[b].coords
        return sum(abs(int(u) - int(v)) for u, v in zip(ca, cb)) == 1

    first = rows[0]
    path = [0]

    def extend():
        if len(path) == size:
            return near(first, path[-1], path[0])
        for nxt in range(size):
            if nxt not in path and near(first, path[-1], nxt):
                path.append(nxt)
                if extend():
                    return True
                path.pop()
        return False

    if not extend():
        return None
    for row in rows:
        if not all(near(row, path[j], path[(j + 1) % size]) for j in range(size)):
            return None
    return tuple(path)


def per_device(ring, latents, spatial_weight, temporal_weight, skip_weight, norm_gain, norm_bias):
    sections = lax.axis_size("segment")
    position = lax.axis_index("segment")
    steps_total = MICRO + sections - 1
    gains = norm_gain[0]
    offsets = norm_bias[0]
    width = spatial_weight.shape[-1]
    micro, samples, frames, rows, cols = latents.shape[:5]
    dims = (samples, frames, rows, cols)
    flat = latents.reshape(micro, -1, width)
    rs, rt = spatial_weight.shape[1], temporal_weight.shape[1]
    pack = jnp.concatenate([spatial_weight[0], temporal_weight[0], skip_weight[0]], axis=0)
    if ring is None:
        gathered = lax.all_gather(pack, "fsdp", axis=0, tiled=False)
    else:
        gathered = ring_gather(pack, "fsdp", ring)
    spatial3 = gathered[:, :rs].reshape(9, width, width)
    temporal3 = gathered[:, rs : rs + rt].reshape(3, width, width)
    skip_mat = gathered[:, rs + rt :].reshape(width, width)
    blank = jnp.zeros_like(flat[0])
    results = [blank] * MICRO
    skips = [None] * MICRO
    previous = blank
    for moment in range(steps_total):
        if moment == 0:
            incoming = blank
        else:
            pairs = [
                (s, s + 1) for s in range(sections - 1) if 0 <= moment - 1 - s < MICRO
            ]
            incoming = lax.ppermute(previous, "segment", pairs)
        fresh = flat[min(moment, MICRO - 1)] if moment < MICRO else blank
        stream = jnp.where(position == 0, fresh, incoming)
        late_index = moment - (sections - 1)
        skip_in = skips[late_index] if 0 <= late_index < MICRO else None
        output = section(stream, skip_in, spatial3, temporal3, skip_mat, gains, offsets, dims)
        which = moment - position
        for slot_index in range(MICRO):
            if 0 <= moment - slot_index < sections:
                results[slot_index] = jnp.where(which == slot_index, output, results[slot_index])
        if moment < MICRO:
            skips[moment] = lax.ppermute(output, "segment", [(0, sections - 1)])
        previous = output
    return jnp.stack(results).reshape((1,) + latents.shape)


def solution(mesh):
    placed = (
        P(None, "fsdp", None, None, None, None),
        P("segment", "fsdp", None),
        P("segment", "fsdp", None),
        P("segment", "fsdp", None),
        P("segment", None, None),
        P("segment", None, None),
    )
    ring = neighbour_ring(mesh, "fsdp")
    return jax.shard_map(
        functools.partial(per_device, ring),
        mesh=mesh,
        in_specs=placed,
        out_specs=P("segment", None, "fsdp", None, None, None, None),
        check_vma=False,
    )
```

```python
import functools

import jax
import jax.numpy as jnp
from jax import lax
from jax.sharding import PartitionSpec as P

GROUPS = 32
MICRO = 2


precise = lax.Precision.HIGH


def group_norm(field, samples, gain, offset):
    width = field.shape[-1]
    grouped = field.reshape(samples, -1, GROUPS, width // GROUPS)
    center = jnp.mean(grouped, axis=(1, 3), keepdims=True)
    spread = jnp.mean((grouped - center) ** 2, axis=(1, 3), keepdims=True)
    normed = ((grouped - center) * lax.rsqrt(spread + 1e-05)).reshape(field.shape)
    return normed * gain + offset


def shifted(field, offset, valid, pad):
    padded = jnp.pad(field, ((pad, pad), (0, 0)))
    rows = field.shape[0]
    piece = padded[pad + offset : pad + offset + rows]
    return jnp.where(valid, piece, jnp.zeros_like(piece))


def spatial_conv(first, spatial3, frames, rows, cols):
    positions = first.shape[0]
    products = jnp.einsum(
        "pc,tco->tpo", first, spatial3, precision=precise, preferred_element_type=jnp.float32
    )
    pos = lax.broadcasted_iota(jnp.int32, (positions, 1), 0)
    within = pos % (rows * cols)
    row = within // cols
    col = within % cols
    total = None
    for delta_row in range(3):
        for delta_col in range(3):
            r = row + delta_row - 1
            c = col + delta_col - 1
            valid = (r >= 0) & (r < rows) & (c >= 0) & (c < cols)
            offset = (delta_row - 1) * cols + (delta_col - 1)
            piece = shifted(products[3 * delta_row + delta_col], offset, valid, cols + 1)
            total = piece if total is None else total + piece
    return total


def temporal_conv(second, temporal3, frames, rows, cols):
    positions = second.shape[0]
    plane = rows * cols
    products = jnp.einsum(
        "pc,tco->tpo", second, temporal3, precision=precise, preferred_element_type=jnp.float32
    )
    pos = lax.broadcasted_iota(jnp.int32, (positions, 1), 0)
    frame = (pos // plane) % frames
    total = None
    for tap in range(3):
        f = frame + tap - 1
        valid = (f >= 0) & (f < frames)
        piece = shifted(products[tap], (tap - 1) * plane, valid, plane)
        total = piece if total is None else total + piece
    return total


def section(x, skip_in, spatial3, temporal3, skip_mat, gains, offsets, dims):
    samples, frames, rows, cols = dims
    if skip_in is None:
        hidden = x
    else:
        hidden = x + jnp.dot(
            skip_in, skip_mat, precision=precise, preferred_element_type=jnp.float32
        )
    first = jax.nn.silu(group_norm(hidden, samples, gains[0], offsets[0]))
    mixed = hidden + spatial_conv(first, spatial3, frames, rows, cols)
    second = jax.nn.silu(group_norm(mixed, samples, gains[1], offsets[1]))
    return mixed + temporal_conv(second, temporal3, frames, rows, cols)


def ring_gather(pack, axis, ring):
    size = len(ring)
    place = [0] * size
    for spot, member in enumerate(ring):
        place[member] = spot
    me = lax.axis_index(axis)
    spot = jnp.array(place, jnp.int32)[me]
    members = jnp.array(ring, jnp.int32)
    out = jnp.zeros((size,) + pack.shape, pack.dtype)
    out = lax.dynamic_update_index_in_dim(out, pack, me, 0)
    ahead = [(ring[j], ring[(j + 1) % size]) for j in range(size)]
    behind = [(ring[(j + 1) % size], ring[j]) for j in range(size)]
    forward = backward = pack
    steps_forward = size // 2
    steps_backward = size - 1 - steps_forward
    for step in range(1, steps_forward + 1):
        forward = lax.ppermute(forward, axis, ahead)
        out = lax.dynamic_update_index_in_dim(out, forward, members[(spot - step) % size], 0)
        if step <= steps_backward:
            backward = lax.ppermute(backward, axis, behind)
            out = lax.dynamic_update_index_in_dim(
                out, backward, members[(spot + step) % size], 0
            )
    return out


def neighbour_ring(mesh, axis):
    names = list(mesh.axis_names)
    where = names.index(axis)
    grid = mesh.devices.transpose([i for i in range(len(names)) if i != where] + [where])
    rows = grid.reshape(-1, grid.shape[-1])
    size = rows.shape[1]
    if size < 3 or size > 16:
        return None

    def near(row, a, b):
        ca, cb = row[a].coords, row[b].coords
        return sum(abs(int(u) - int(v)) for u, v in zip(ca, cb)) == 1

    first = rows[0]
    path = [0]

    def extend():
        if len(path) == size:
            return near(first, path[-1], path[0])
        for nxt in range(size):
            if nxt not in path and near(first, path[-1], nxt):
                path.append(nxt)
                if extend():
                    return True
                path.pop()
        return False

    if not extend():
        return None
    for row in rows:
        if not all(near(row, path[j], path[(j + 1) % size]) for j in range(size)):
            return None
    return tuple(path)


def per_device(ring, latents, spatial_weight, temporal_weight, skip_weight, norm_gain, norm_bias):
    sections = lax.axis_size("segment")
    position = lax.axis_index("segment")
    steps_total = MICRO + sections - 1
    gains = norm_gain[0]
    offsets = norm_bias[0]
    width = spatial_weight.shape[-1]
    micro, samples, frames, rows, cols = latents.shape[:5]
    dims = (samples, frames, rows, cols)
    flat = latents.reshape(micro, -1, width)
    rs, rt = spatial_weight.shape[1], temporal_weight.shape[1]
    pack = jnp.concatenate([spatial_weight[0], temporal_weight[0], skip_weight[0]], axis=0)
    if ring is None:
        gathered = lax.all_gather(pack, "fsdp", axis=0, tiled=False)
    else:
        gathered = ring_gather(pack, "fsdp", ring)
    spatial3 = gathered[:, :rs].reshape(9, width, width)
    temporal3 = gathered[:, rs : rs + rt].reshape(3, width, width)
    skip_mat = gathered[:, rs + rt :].reshape(width, width)
    blank = jnp.zeros_like(flat[0])
    results = [blank] * MICRO
    skips = [None] * MICRO
    previous = blank
    pending = None
    for moment in range(steps_total):
        if moment == 0:
            incoming = blank
        else:
            pairs = [
                (s, s + 1) for s in range(sections - 1) if 0 <= moment - 1 - s < MICRO
            ]
            incoming = lax.ppermute(previous, "segment", pairs)
        sending = None
        if pending is not None:
            payload, incoming = lax.optimization_barrier((pending, incoming))
            sending = moment - 1
            skips[sending] = lax.ppermute(payload, "segment", [(0, sections - 1)])
            pending = None
        fresh = flat[min(moment, MICRO - 1)] if moment < MICRO else blank
        stream = jnp.where(position == 0, fresh, incoming)
        late_index = moment - (sections - 1)
        skip_in = skips[late_index] if 0 <= late_index < MICRO else None
        output = section(stream, skip_in, spatial3, temporal3, skip_mat, gains, offsets, dims)
        if sending is not None:
            skips[sending], output = lax.optimization_barrier((skips[sending], output))
        which = moment - position
        for slot_index in range(MICRO):
            results[slot_index] = jnp.where(which == slot_index, output, results[slot_index])
        if moment < MICRO:
            pending = output
        previous = output
    return jnp.stack(results).reshape((1,) + latents.shape)


def solution(mesh):
    placed = (
        P(None, "fsdp", None, None, None, None),
        P("segment", "fsdp", None),
        P("segment", "fsdp", None),
        P("segment", "fsdp", None),
        P("segment", None, None),
        P("segment", None, None),
    )
    ring = neighbour_ring(mesh, "fsdp")
    return jax.shard_map(
        functools.partial(per_device, ring),
        mesh=mesh,
        in_specs=placed,
        out_specs=P("segment", None, "fsdp", None, None, None, None),
        check_vma=False,
    )
```

```python
import functools

import jax
import jax.numpy as jnp
from jax import lax
from jax.sharding import PartitionSpec as P

GROUPS = 32
MICRO = 2


precise = lax.Precision.HIGH


def group_norm(field, samples, gain, offset):
    width = field.shape[-1]
    grouped = field.reshape(samples, -1, GROUPS, width // GROUPS)
    center = jnp.mean(grouped, axis=(1, 3), keepdims=True)
    spread = jnp.mean((grouped - center) ** 2, axis=(1, 3), keepdims=True)
    normed = ((grouped - center) * lax.rsqrt(spread + 1e-05)).reshape(field.shape)
    return normed * gain + offset


def shifted(field, offset, valid, pad):
    padded = jnp.pad(field, ((pad, pad), (0, 0)))
    rows = field.shape[0]
    piece = padded[pad + offset : pad + offset + rows]
    return jnp.where(valid, piece, jnp.zeros_like(piece))


def spatial_conv(first, spatial3, frames, rows, cols):
    positions = first.shape[0]
    products = jnp.einsum(
        "pc,tco->tpo", first, spatial3, precision=precise, preferred_element_type=jnp.float32
    )
    pos = lax.broadcasted_iota(jnp.int32, (positions, 1), 0)
    within = pos % (rows * cols)
    row = within // cols
    col = within % cols
    total = None
    for delta_row in range(3):
        for delta_col in range(3):
            r = row + delta_row - 1
            c = col + delta_col - 1
            valid = (r >= 0) & (r < rows) & (c >= 0) & (c < cols)
            offset = (delta_row - 1) * cols + (delta_col - 1)
            piece = shifted(products[3 * delta_row + delta_col], offset, valid, cols + 1)
            total = piece if total is None else total + piece
    return total


def temporal_conv(second, temporal3, frames, rows, cols):
    positions = second.shape[0]
    plane = rows * cols
    products = jnp.einsum(
        "pc,tco->tpo", second, temporal3, precision=precise, preferred_element_type=jnp.float32
    )
    pos = lax.broadcasted_iota(jnp.int32, (positions, 1), 0)
    frame = (pos // plane) % frames
    total = None
    for tap in range(3):
        f = frame + tap - 1
        valid = (f >= 0) & (f < frames)
        piece = shifted(products[tap], (tap - 1) * plane, valid, plane)
        total = piece if total is None else total + piece
    return total


def section(x, skip_in, spatial3, temporal3, skip_mat, gains, offsets, dims):
    samples, frames, rows, cols = dims
    if skip_in is None:
        hidden = x
    else:
        hidden = x + jnp.dot(
            skip_in, skip_mat, precision=precise, preferred_element_type=jnp.float32
        )
    first = jax.nn.silu(group_norm(hidden, samples, gains[0], offsets[0]))
    mixed = hidden + spatial_conv(first, spatial3, frames, rows, cols)
    second = jax.nn.silu(group_norm(mixed, samples, gains[1], offsets[1]))
    return mixed + temporal_conv(second, temporal3, frames, rows, cols)


def ring_gather(pack, axis, ring):
    size = len(ring)
    place = [0] * size
    for spot, member in enumerate(ring):
        place[member] = spot
    me = lax.axis_index(axis)
    spot = jnp.array(place, jnp.int32)[me]
    members = jnp.array(ring, jnp.int32)
    out = jnp.zeros((size,) + pack.shape, pack.dtype)
    out = lax.dynamic_update_index_in_dim(out, pack, me, 0)
    ahead = [(ring[j], ring[(j + 1) % size]) for j in range(size)]
    behind = [(ring[(j + 1) % size], ring[j]) for j in range(size)]
    forward = backward = pack
    steps_forward = size // 2
    steps_backward = size - 1 - steps_forward
    for step in range(1, steps_forward + 1):
        forward = lax.ppermute(forward, axis, ahead)
        out = lax.dynamic_update_index_in_dim(out, forward, members[(spot - step) % size], 0)
        if step <= steps_backward:
            backward = lax.ppermute(backward, axis, behind)
            out = lax.dynamic_update_index_in_dim(
                out, backward, members[(spot + step) % size], 0
            )
    return out


def neighbour_ring(mesh, axis):
    names = list(mesh.axis_names)
    where = names.index(axis)
    grid = mesh.devices.transpose([i for i in range(len(names)) if i != where] + [where])
    rows = grid.reshape(-1, grid.shape[-1])
    size = rows.shape[1]
    if size < 3 or size > 16:
        return None

    def near(row, a, b):
        ca, cb = row[a].coords, row[b].coords
        return sum(abs(int(u) - int(v)) for u, v in zip(ca, cb)) == 1

    first = rows[0]
    path = [0]

    def extend():
        if len(path) == size:
            return near(first, path[-1], path[0])
        for nxt in range(size):
            if nxt not in path and near(first, path[-1], nxt):
                path.append(nxt)
                if extend():
                    return True
                path.pop()
        return False

    if not extend():
        return None
    for row in rows:
        if not all(near(row, path[j], path[(j + 1) % size]) for j in range(size)):
            return None
    return tuple(path)


def per_device(ring, latents, spatial_weight, temporal_weight, skip_weight, norm_gain, norm_bias):
    sections = lax.axis_size("segment")
    position = lax.axis_index("segment")
    steps_total = MICRO + sections - 1
    gains = norm_gain[0]
    offsets = norm_bias[0]
    width = spatial_weight.shape[-1]
    micro, samples, frames, rows, cols = latents.shape[:5]
    dims = (samples, frames, rows, cols)
    flat = latents.reshape(micro, -1, width)
    rs, rt = spatial_weight.shape[1], temporal_weight.shape[1]
    pack = jnp.concatenate([spatial_weight[0], temporal_weight[0], skip_weight[0]], axis=0)
    if ring is None:
        gathered = lax.all_gather(pack, "fsdp", axis=0, tiled=False)
    else:
        gathered = ring_gather(pack, "fsdp", ring)
    spatial3 = gathered[:, :rs].reshape(9, width, width)
    temporal3 = gathered[:, rs : rs + rt].reshape(3, width, width)
    skip_mat = gathered[:, rs + rt :].reshape(width, width)
    blank = jnp.zeros_like(flat[0])
    results = [blank] * MICRO
    skips = [None] * MICRO
    previous = blank
    for moment in range(steps_total):
        if moment == 0:
            incoming = blank
        else:
            pairs = [
                (s, s + 1) for s in range(sections - 1) if 0 <= moment - 1 - s < MICRO
            ]
            incoming = blank
            for source, target in pairs:
                got = lax.ppermute(previous, "segment", [(source, target)])
                incoming = jnp.where(position == target, got, incoming)
        fresh = flat[min(moment, MICRO - 1)] if moment < MICRO else blank
        stream = jnp.where(position == 0, fresh, incoming)
        late_index = moment - (sections - 1)
        skip_in = skips[late_index] if 0 <= late_index < MICRO else None
        output = section(stream, skip_in, spatial3, temporal3, skip_mat, gains, offsets, dims)
        which = moment - position
        for slot_index in range(MICRO):
            results[slot_index] = jnp.where(which == slot_index, output, results[slot_index])
        if moment < MICRO:
            skips[moment] = lax.ppermute(output, "segment", [(0, sections - 1)])
        previous = output
    return jnp.stack(results).reshape((1,) + latents.shape)


def solution(mesh):
    placed = (
        P(None, "fsdp", None, None, None, None),
        P("segment", "fsdp", None),
        P("segment", "fsdp", None),
        P("segment", "fsdp", None),
        P("segment", None, None),
        P("segment", None, None),
    )
    ring = neighbour_ring(mesh, "fsdp")
    return jax.shard_map(
        functools.partial(per_device, ring),
        mesh=mesh,
        in_specs=placed,
        out_specs=P("segment", None, "fsdp", None, None, None, None),
        check_vma=False,
    )
```

```python
import functools

import jax
import jax.numpy as jnp
from jax import lax
from jax.sharding import PartitionSpec as P

GROUPS = 32
MICRO = 2


precise = lax.Precision.HIGH


def group_norm(field, samples, gain, offset):
    width = field.shape[-1]
    grouped = field.reshape(samples, -1, GROUPS, width // GROUPS)
    center = jnp.mean(grouped, axis=(1, 3), keepdims=True)
    spread = jnp.mean((grouped - center) ** 2, axis=(1, 3), keepdims=True)
    normed = ((grouped - center) * lax.rsqrt(spread + 1e-05)).reshape(field.shape)
    return normed * gain + offset


def shifted(field, offset, valid, pad):
    padded = jnp.pad(field, ((pad, pad), (0, 0)))
    rows = field.shape[0]
    piece = padded[pad + offset : pad + offset + rows]
    return jnp.where(valid, piece, jnp.zeros_like(piece))


def spatial_conv(first, spatial3, frames, rows, cols):
    positions = first.shape[0]
    products = jnp.einsum(
        "pc,tco->tpo", first, spatial3, precision=precise, preferred_element_type=jnp.float32
    )
    pos = lax.broadcasted_iota(jnp.int32, (positions, 1), 0)
    within = pos % (rows * cols)
    row = within // cols
    col = within % cols
    total = None
    for delta_row in range(3):
        for delta_col in range(3):
            r = row + delta_row - 1
            c = col + delta_col - 1
            valid = (r >= 0) & (r < rows) & (c >= 0) & (c < cols)
            offset = (delta_row - 1) * cols + (delta_col - 1)
            piece = shifted(products[3 * delta_row + delta_col], offset, valid, cols + 1)
            total = piece if total is None else total + piece
    return total


def temporal_conv(second, temporal3, frames, rows, cols):
    positions = second.shape[0]
    plane = rows * cols
    products = jnp.einsum(
        "pc,tco->tpo", second, temporal3, precision=precise, preferred_element_type=jnp.float32
    )
    pos = lax.broadcasted_iota(jnp.int32, (positions, 1), 0)
    frame = (pos // plane) % frames
    total = None
    for tap in range(3):
        f = frame + tap - 1
        valid = (f >= 0) & (f < frames)
        piece = shifted(products[tap], (tap - 1) * plane, valid, plane)
        total = piece if total is None else total + piece
    return total


def section(x, skip_in, spatial3, temporal3, skip_mat, gains, offsets, dims):
    samples, frames, rows, cols = dims
    if skip_in is None:
        hidden = x
    else:
        hidden = x + jnp.dot(
            skip_in, skip_mat, precision=precise, preferred_element_type=jnp.float32
        )
    first = jax.nn.silu(group_norm(hidden, samples, gains[0], offsets[0]))
    mixed = hidden + spatial_conv(first, spatial3, frames, rows, cols)
    second = jax.nn.silu(group_norm(mixed, samples, gains[1], offsets[1]))
    return mixed + temporal_conv(second, temporal3, frames, rows, cols)


def ring_gather(pack, axis, ring):
    size = len(ring)
    place = [0] * size
    for spot, member in enumerate(ring):
        place[member] = spot
    me = lax.axis_index(axis)
    spot = jnp.array(place, jnp.int32)[me]
    members = jnp.array(ring, jnp.int32)
    out = jnp.zeros((size,) + pack.shape, pack.dtype)
    out = lax.dynamic_update_index_in_dim(out, pack, me, 0)
    ahead = [(ring[j], ring[(j + 1) % size]) for j in range(size)]
    behind = [(ring[(j + 1) % size], ring[j]) for j in range(size)]
    forward = backward = pack
    steps_forward = size // 2
    steps_backward = size - 1 - steps_forward
    for step in range(1, steps_forward + 1):
        forward = lax.ppermute(forward, axis, ahead)
        out = lax.dynamic_update_index_in_dim(out, forward, members[(spot - step) % size], 0)
        if step <= steps_backward:
            backward = lax.ppermute(backward, axis, behind)
            out = lax.dynamic_update_index_in_dim(
                out, backward, members[(spot + step) % size], 0
            )
    return out


def neighbour_ring(mesh, axis):
    names = list(mesh.axis_names)
    where = names.index(axis)
    grid = mesh.devices.transpose([i for i in range(len(names)) if i != where] + [where])
    rows = grid.reshape(-1, grid.shape[-1])
    size = rows.shape[1]
    if size < 3 or size > 16:
        return None

    def near(row, a, b):
        ca, cb = row[a].coords, row[b].coords
        return sum(abs(int(u) - int(v)) for u, v in zip(ca, cb)) == 1

    first = rows[0]
    path = [0]

    def extend():
        if len(path) == size:
            return near(first, path[-1], path[0])
        for nxt in range(size):
            if nxt not in path and near(first, path[-1], nxt):
                path.append(nxt)
                if extend():
                    return True
                path.pop()
        return False

    if not extend():
        return None
    for row in rows:
        if not all(near(row, path[j], path[(j + 1) % size]) for j in range(size)):
            return None
    return tuple(path)


def per_device(ring, latents, spatial_weight, temporal_weight, skip_weight, norm_gain, norm_bias):
    sections = lax.axis_size("segment")
    position = lax.axis_index("segment")
    steps_total = MICRO + sections - 1
    gains = norm_gain[0]
    offsets = norm_bias[0]
    width = spatial_weight.shape[-1]
    micro, samples, frames, rows, cols = latents.shape[:5]
    dims = (samples, frames, rows, cols)
    flat = latents.reshape(micro, -1, width)
    rs, rt = spatial_weight.shape[1], temporal_weight.shape[1]
    pack = jnp.concatenate([spatial_weight[0], temporal_weight[0], skip_weight[0]], axis=0)
    if ring is None:
        gathered = lax.all_gather(pack, "fsdp", axis=0, tiled=False)
    else:
        gathered = ring_gather(pack, "fsdp", ring)
    spatial3 = gathered[:, :rs].reshape(9, width, width)
    temporal3 = gathered[:, rs : rs + rt].reshape(3, width, width)
    skip_mat = gathered[:, rs + rt :].reshape(width, width)
    blank = jnp.zeros_like(flat[0])
    outputs = []
    skips = [None] * MICRO
    previous = blank
    for moment in range(steps_total):
        if moment == 0:
            incoming = blank
        else:
            pairs = [
                (s, s + 1) for s in range(sections - 1) if 0 <= moment - 1 - s < MICRO
            ]
            incoming = lax.ppermute(previous, "segment", pairs)
        fresh = flat[min(moment, MICRO - 1)] if moment < MICRO else blank
        stream = jnp.where(position == 0, fresh, incoming)
        late_index = moment - (sections - 1)
        skip_in = skips[late_index] if 0 <= late_index < MICRO else None
        output = section(stream, skip_in, spatial3, temporal3, skip_mat, gains, offsets, dims)
        outputs.append(output)
        if moment < MICRO:
            skips[moment] = lax.ppermute(output, "segment", [(0, sections - 1)])
        previous = output
    held = lax.dynamic_slice_in_dim(jnp.stack(outputs), position, MICRO, axis=0)
    return held.reshape((1,) + latents.shape)


def solution(mesh):
    placed = (
        P(None, "fsdp", None, None, None, None),
        P("segment", "fsdp", None),
        P("segment", "fsdp", None),
        P("segment", "fsdp", None),
        P("segment", None, None),
        P("segment", None, None),
    )
    ring = neighbour_ring(mesh, "fsdp")
    return jax.shard_map(
        functools.partial(per_device, ring),
        mesh=mesh,
        in_specs=placed,
        out_specs=P("segment", None, "fsdp", None, None, None, None),
        check_vma=False,
    )
```

```python
import functools

import jax
import jax.numpy as jnp
from jax import lax
from jax.sharding import PartitionSpec as P

GROUPS = 32
MICRO = 2


precise = lax.Precision.HIGH


def group_norm(field, samples, gain, offset):
    width = field.shape[-1]
    grouped = field.reshape(samples, -1, GROUPS, width // GROUPS)
    center = jnp.mean(grouped, axis=(1, 3), keepdims=True)
    spread = jnp.mean((grouped - center) ** 2, axis=(1, 3), keepdims=True)
    normed = ((grouped - center) * lax.rsqrt(spread + 1e-05)).reshape(field.shape)
    return normed * gain + offset


def shifted(field, offset, valid, pad):
    padded = jnp.pad(field, ((pad, pad), (0, 0)))
    rows = field.shape[0]
    piece = padded[pad + offset : pad + offset + rows]
    return jnp.where(valid, piece, jnp.zeros_like(piece))


def spatial_conv(first, spatial3, frames, rows, cols):
    positions = first.shape[0]
    products = jnp.einsum(
        "pc,tco->tpo", first, spatial3, precision=precise, preferred_element_type=jnp.float32
    )
    pos = lax.broadcasted_iota(jnp.int32, (positions, 1), 0)
    within = pos % (rows * cols)
    row = within // cols
    col = within % cols
    total = None
    for delta_row in range(3):
        for delta_col in range(3):
            r = row + delta_row - 1
            c = col + delta_col - 1
            valid = (r >= 0) & (r < rows) & (c >= 0) & (c < cols)
            offset = (delta_row - 1) * cols + (delta_col - 1)
            piece = shifted(products[3 * delta_row + delta_col], offset, valid, cols + 1)
            total = piece if total is None else total + piece
    return total


def temporal_conv(second, temporal3, frames, rows, cols):
    positions = second.shape[0]
    plane = rows * cols
    products = jnp.einsum(
        "pc,tco->tpo", second, temporal3, precision=precise, preferred_element_type=jnp.float32
    )
    pos = lax.broadcasted_iota(jnp.int32, (positions, 1), 0)
    frame = (pos // plane) % frames
    total = None
    for tap in range(3):
        f = frame + tap - 1
        valid = (f >= 0) & (f < frames)
        piece = shifted(products[tap], (tap - 1) * plane, valid, plane)
        total = piece if total is None else total + piece
    return total


def section(x, skip_in, spatial3, temporal3, skip_mat, gains, offsets, dims):
    samples, frames, rows, cols = dims
    if skip_in is None:
        hidden = x
    else:
        hidden = x + jnp.dot(
            skip_in, skip_mat, precision=precise, preferred_element_type=jnp.float32
        )
    first = jax.nn.silu(group_norm(hidden, samples, gains[0], offsets[0]))
    mixed = hidden + spatial_conv(first, spatial3, frames, rows, cols)
    second = jax.nn.silu(group_norm(mixed, samples, gains[1], offsets[1]))
    return mixed + temporal_conv(second, temporal3, frames, rows, cols)


def ring_gather(pack, axis, ring):
    size = len(ring)
    place = [0] * size
    for spot, member in enumerate(ring):
        place[member] = spot
    me = lax.axis_index(axis)
    spot = jnp.array(place, jnp.int32)[me]
    members = jnp.array(ring, jnp.int32)
    out = jnp.zeros((size,) + pack.shape, pack.dtype)
    out = lax.dynamic_update_index_in_dim(out, pack, me, 0)
    ahead = [(ring[j], ring[(j + 1) % size]) for j in range(size)]
    behind = [(ring[(j + 1) % size], ring[j]) for j in range(size)]
    forward = backward = pack
    steps_forward = size // 2
    steps_backward = size - 1 - steps_forward
    for step in range(1, steps_forward + 1):
        forward = lax.ppermute(forward, axis, ahead)
        out = lax.dynamic_update_index_in_dim(out, forward, members[(spot - step) % size], 0)
        if step <= steps_backward:
            backward = lax.ppermute(backward, axis, behind)
            out = lax.dynamic_update_index_in_dim(
                out, backward, members[(spot + step) % size], 0
            )
    return out


def neighbour_ring(mesh, axis):
    names = list(mesh.axis_names)
    where = names.index(axis)
    grid = mesh.devices.transpose([i for i in range(len(names)) if i != where] + [where])
    rows = grid.reshape(-1, grid.shape[-1])
    size = rows.shape[1]
    if size < 3 or size > 16:
        return None

    def near(row, a, b):
        ca, cb = row[a].coords, row[b].coords
        return sum(abs(int(u) - int(v)) for u, v in zip(ca, cb)) == 1

    first = rows[0]
    path = [0]

    def extend():
        if len(path) == size:
            return near(first, path[-1], path[0])
        for nxt in range(size):
            if nxt not in path and near(first, path[-1], nxt):
                path.append(nxt)
                if extend():
                    return True
                path.pop()
        return False

    if not extend():
        return None
    for row in rows:
        if not all(near(row, path[j], path[(j + 1) % size]) for j in range(size)):
            return None
    return tuple(path)


def per_device(ring, latents, spatial_weight, temporal_weight, skip_weight, norm_gain, norm_bias):
    sections = lax.axis_size("segment")
    position = lax.axis_index("segment")
    steps_total = MICRO + sections - 1
    gains = norm_gain[0]
    offsets = norm_bias[0]
    width = spatial_weight.shape[-1]
    micro, samples, frames, rows, cols = latents.shape[:5]
    dims = (samples, frames, rows, cols)
    flat = latents.reshape(micro, -1, width)
    rs, rt = spatial_weight.shape[1], temporal_weight.shape[1]
    pack = jnp.concatenate([spatial_weight[0], temporal_weight[0], skip_weight[0]], axis=0)
    if ring is None:
        gathered = lax.all_gather(pack, "fsdp", axis=0, tiled=False)
    else:
        gathered = ring_gather(pack, "fsdp", ring)
    spatial3 = gathered[:, :rs].reshape(9, width, width)
    temporal3 = gathered[:, rs : rs + rt].reshape(3, width, width)
    skip_mat = gathered[:, rs + rt :].reshape(width, width)
    blank = jnp.zeros_like(flat[0])
    outputs = []
    skips = [None] * MICRO
    previous = blank
    for moment in range(steps_total):
        if moment == 0:
            incoming = blank
        else:
            pairs = [
                (s, s + 1) for s in range(sections - 1) if 0 <= moment - 1 - s < MICRO
            ]
            incoming = lax.ppermute(previous, "segment", pairs)
            stored, incoming = lax.optimization_barrier((previous, incoming))
            outputs.append(stored)
        fresh = flat[min(moment, MICRO - 1)] if moment < MICRO else blank
        stream = jnp.where(position == 0, fresh, incoming)
        late_index = moment - (sections - 1)
        skip_in = skips[late_index] if 0 <= late_index < MICRO else None
        output = section(stream, skip_in, spatial3, temporal3, skip_mat, gains, offsets, dims)
        if moment < MICRO:
            skips[moment] = lax.ppermute(output, "segment", [(0, sections - 1)])
        previous = output
    outputs.append(previous)
    held = lax.dynamic_slice_in_dim(jnp.stack(outputs), position, MICRO, axis=0)
    return held.reshape((1,) + latents.shape)


def solution(mesh):
    placed = (
        P(None, "fsdp", None, None, None, None),
        P("segment", "fsdp", None),
        P("segment", "fsdp", None),
        P("segment", "fsdp", None),
        P("segment", None, None),
        P("segment", None, None),
    )
    ring = neighbour_ring(mesh, "fsdp")
    return jax.shard_map(
        functools.partial(per_device, ring),
        mesh=mesh,
        in_specs=placed,
        out_specs=P("segment", None, "fsdp", None, None, None, None),
        check_vma=False,
    )
```

```python
import functools

import jax
import jax.numpy as jnp
from jax import lax
from jax.sharding import PartitionSpec as P

GROUPS = 32
MICRO = 2


precise = lax.Precision.HIGH


def group_norm(field, samples, gain, offset):
    width = field.shape[-1]
    grouped = field.reshape(samples, -1, GROUPS, width // GROUPS)
    center = jnp.mean(grouped, axis=(1, 3), keepdims=True)
    spread = jnp.mean((grouped - center) ** 2, axis=(1, 3), keepdims=True)
    normed = ((grouped - center) * lax.rsqrt(spread + 1e-05)).reshape(field.shape)
    return normed * gain + offset


def shifted(field, offset, valid, pad):
    padded = jnp.pad(field, ((pad, pad), (0, 0)))
    rows = field.shape[0]
    piece = padded[pad + offset : pad + offset + rows]
    return jnp.where(valid, piece, jnp.zeros_like(piece))


def spatial_conv(first, spatial3, frames, rows, cols):
    positions = first.shape[0]
    products = jnp.einsum(
        "pc,tco->tpo", first, spatial3, precision=precise, preferred_element_type=jnp.float32
    )
    pos = lax.broadcasted_iota(jnp.int32, (positions, 1), 0)
    within = pos % (rows * cols)
    row = within // cols
    col = within % cols
    total = None
    for delta_row in range(3):
        for delta_col in range(3):
            r = row + delta_row - 1
            c = col + delta_col - 1
            valid = (r >= 0) & (r < rows) & (c >= 0) & (c < cols)
            offset = (delta_row - 1) * cols + (delta_col - 1)
            piece = shifted(products[3 * delta_row + delta_col], offset, valid, cols + 1)
            total = piece if total is None else total + piece
    return total


def temporal_conv(second, temporal3, frames, rows, cols):
    positions = second.shape[0]
    plane = rows * cols
    products = jnp.einsum(
        "pc,tco->tpo", second, temporal3, precision=precise, preferred_element_type=jnp.float32
    )
    pos = lax.broadcasted_iota(jnp.int32, (positions, 1), 0)
    frame = (pos // plane) % frames
    total = None
    for tap in range(3):
        f = frame + tap - 1
        valid = (f >= 0) & (f < frames)
        piece = shifted(products[tap], (tap - 1) * plane, valid, plane)
        total = piece if total is None else total + piece
    return total


def section(x, skip_in, spatial3, temporal3, skip_mat, gains, offsets, dims):
    samples, frames, rows, cols = dims
    if skip_in is None:
        hidden = x
    else:
        hidden = x + jnp.dot(
            skip_in, skip_mat, precision=precise, preferred_element_type=jnp.float32
        )
    first = jax.nn.silu(group_norm(hidden, samples, gains[0], offsets[0]))
    mixed = hidden + spatial_conv(first, spatial3, frames, rows, cols)
    second = jax.nn.silu(group_norm(mixed, samples, gains[1], offsets[1]))
    return mixed + temporal_conv(second, temporal3, frames, rows, cols)


def ring_gather(pack, axis, ring):
    size = len(ring)
    place = [0] * size
    for spot, member in enumerate(ring):
        place[member] = spot
    me = lax.axis_index(axis)
    spot = jnp.array(place, jnp.int32)[me]
    members = jnp.array(ring, jnp.int32)
    out = jnp.zeros((size,) + pack.shape, pack.dtype)
    out = lax.dynamic_update_index_in_dim(out, pack, me, 0)
    ahead = [(ring[j], ring[(j + 1) % size]) for j in range(size)]
    behind = [(ring[(j + 1) % size], ring[j]) for j in range(size)]
    forward = backward = pack
    steps_forward = size // 2
    steps_backward = size - 1 - steps_forward
    for step in range(1, steps_forward + 1):
        forward = lax.ppermute(forward, axis, ahead)
        out = lax.dynamic_update_index_in_dim(out, forward, members[(spot - step) % size], 0)
        if step <= steps_backward:
            backward = lax.ppermute(backward, axis, behind)
            out = lax.dynamic_update_index_in_dim(
                out, backward, members[(spot + step) % size], 0
            )
    return out


def neighbour_ring(mesh, axis):
    names = list(mesh.axis_names)
    where = names.index(axis)
    grid = mesh.devices.transpose([i for i in range(len(names)) if i != where] + [where])
    rows = grid.reshape(-1, grid.shape[-1])
    size = rows.shape[1]
    if size < 3 or size > 16:
        return None

    def near(row, a, b):
        ca, cb = row[a].coords, row[b].coords
        return sum(abs(int(u) - int(v)) for u, v in zip(ca, cb)) == 1

    first = rows[0]
    path = [0]

    def extend():
        if len(path) == size:
            return near(first, path[-1], path[0])
        for nxt in range(size):
            if nxt not in path and near(first, path[-1], nxt):
                path.append(nxt)
                if extend():
                    return True
                path.pop()
        return False

    if not extend():
        return None
    for row in rows:
        if not all(near(row, path[j], path[(j + 1) % size]) for j in range(size)):
            return None
    return tuple(path)


def per_device(ring, latents, spatial_weight, temporal_weight, skip_weight, norm_gain, norm_bias):
    sections = lax.axis_size("segment")
    position = lax.axis_index("segment")
    steps_total = MICRO + sections - 1
    gains = norm_gain[0]
    offsets = norm_bias[0]
    width = spatial_weight.shape[-1]
    micro, samples, frames, rows, cols = latents.shape[:5]
    dims = (samples, frames, rows, cols)
    flat = latents.reshape(micro, -1, width)
    rs, rt = spatial_weight.shape[1], temporal_weight.shape[1]
    pack = jnp.concatenate([spatial_weight[0], temporal_weight[0], skip_weight[0]], axis=0)
    if ring is None:
        gathered = lax.all_gather(pack, "fsdp", axis=0, tiled=False)
    else:
        gathered = ring_gather(pack, "fsdp", ring)
    spatial3 = gathered[:, :rs].reshape(9, width, width)
    temporal3 = gathered[:, rs : rs + rt].reshape(3, width, width)
    skip_mat = gathered[:, rs + rt :].reshape(width, width)
    blank = jnp.zeros_like(flat[0])
    outputs = []
    skips = [None] * MICRO
    previous = blank
    for moment in range(steps_total):
        if moment == 0:
            stream = flat[0]
        else:
            pairs = [
                (s, s + 1) for s in range(sections - 1) if 0 <= moment - 1 - s < MICRO
            ]
            incoming = lax.ppermute(previous, "segment", pairs)
            if moment < MICRO:
                stream = jnp.where(position == 0, flat[moment], incoming)
            else:
                stream = incoming
        late_index = moment - (sections - 1)
        skip_in = skips[late_index] if 0 <= late_index < MICRO else None
        output = section(stream, skip_in, spatial3, temporal3, skip_mat, gains, offsets, dims)
        outputs.append(output)
        if moment < MICRO:
            skips[moment] = lax.ppermute(output, "segment", [(0, sections - 1)])
        previous = output
    held = lax.dynamic_slice_in_dim(jnp.stack(outputs), position, MICRO, axis=0)
    return held.reshape((1,) + latents.shape)


def solution(mesh):
    placed = (
        P(None, "fsdp", None, None, None, None),
        P("segment", "fsdp", None),
        P("segment", "fsdp", None),
        P("segment", "fsdp", None),
        P("segment", None, None),
        P("segment", None, None),
    )
    ring = neighbour_ring(mesh, "fsdp")
    return jax.shard_map(
        functools.partial(per_device, ring),
        mesh=mesh,
        in_specs=placed,
        out_specs=P("segment", None, "fsdp", None, None, None, None),
        check_vma=False,
    )
```

```python
import functools

import jax
import jax.numpy as jnp
from jax import lax
from jax.sharding import PartitionSpec as P

GROUPS = 32
MICRO = 2


precise = lax.Precision.HIGH


def group_norm(field, samples, gain, offset):
    width = field.shape[-1]
    grouped = field.reshape(samples, -1, GROUPS, width // GROUPS)
    center = jnp.mean(grouped, axis=(1, 3), keepdims=True)
    spread = jnp.mean((grouped - center) ** 2, axis=(1, 3), keepdims=True)
    normed = ((grouped - center) * lax.rsqrt(spread + 1e-05)).reshape(field.shape)
    return normed * gain + offset


def shifted(field, offset, valid, pad):
    padded = jnp.pad(field, ((pad, pad), (0, 0)))
    rows = field.shape[0]
    piece = padded[pad + offset : pad + offset + rows]
    return jnp.where(valid, piece, jnp.zeros_like(piece))


def spatial_conv(first, spatial3, frames, rows, cols):
    positions = first.shape[0]
    products = jnp.einsum(
        "pc,tco->tpo", first, spatial3, precision=precise, preferred_element_type=jnp.float32
    )
    pos = lax.broadcasted_iota(jnp.int32, (positions, 1), 0)
    within = pos % (rows * cols)
    row = within // cols
    col = within % cols
    total = None
    for delta_row in range(3):
        for delta_col in range(3):
            r = row + delta_row - 1
            c = col + delta_col - 1
            valid = (r >= 0) & (r < rows) & (c >= 0) & (c < cols)
            offset = (delta_row - 1) * cols + (delta_col - 1)
            piece = shifted(products[3 * delta_row + delta_col], offset, valid, cols + 1)
            total = piece if total is None else total + piece
    return total


def temporal_conv(second, temporal3, frames, rows, cols):
    positions = second.shape[0]
    plane = rows * cols
    products = jnp.einsum(
        "pc,tco->tpo", second, temporal3, precision=precise, preferred_element_type=jnp.float32
    )
    pos = lax.broadcasted_iota(jnp.int32, (positions, 1), 0)
    frame = (pos // plane) % frames
    total = None
    for tap in range(3):
        f = frame + tap - 1
        valid = (f >= 0) & (f < frames)
        piece = shifted(products[tap], (tap - 1) * plane, valid, plane)
        total = piece if total is None else total + piece
    return total


def section(x, skip_in, spatial3, temporal3, skip_mat, gains, offsets, dims):
    samples, frames, rows, cols = dims
    if skip_in is None:
        hidden = x
    else:
        hidden = x + jnp.dot(
            skip_in, skip_mat, precision=precise, preferred_element_type=jnp.float32
        )
    first = jax.nn.silu(group_norm(hidden, samples, gains[0], offsets[0]))
    mixed = hidden + spatial_conv(first, spatial3, frames, rows, cols)
    second = jax.nn.silu(group_norm(mixed, samples, gains[1], offsets[1]))
    return mixed + temporal_conv(second, temporal3, frames, rows, cols)


def ring_gather(pack, axis, ring):
    size = len(ring)
    place = [0] * size
    for spot, member in enumerate(ring):
        place[member] = spot
    me = lax.axis_index(axis)
    spot = jnp.array(place, jnp.int32)[me]
    members = jnp.array(ring, jnp.int32)
    out = jnp.zeros((size,) + pack.shape, pack.dtype)
    out = lax.dynamic_update_index_in_dim(out, pack, me, 0)
    ahead = [(ring[j], ring[(j + 1) % size]) for j in range(size)]
    behind = [(ring[(j + 1) % size], ring[j]) for j in range(size)]
    forward = backward = pack
    steps_forward = size // 2
    steps_backward = size - 1 - steps_forward
    for step in range(1, steps_forward + 1):
        forward = lax.ppermute(forward, axis, ahead)
        out = lax.dynamic_update_index_in_dim(out, forward, members[(spot - step) % size], 0)
        if step <= steps_backward:
            backward = lax.ppermute(backward, axis, behind)
            out = lax.dynamic_update_index_in_dim(
                out, backward, members[(spot + step) % size], 0
            )
    return out


def neighbour_ring(mesh, axis):
    names = list(mesh.axis_names)
    where = names.index(axis)
    grid = mesh.devices.transpose([i for i in range(len(names)) if i != where] + [where])
    rows = grid.reshape(-1, grid.shape[-1])
    size = rows.shape[1]
    if size < 3 or size > 16:
        return None

    def near(row, a, b):
        ca, cb = row[a].coords, row[b].coords
        return sum(abs(int(u) - int(v)) for u, v in zip(ca, cb)) == 1

    first = rows[0]
    path = [0]

    def extend():
        if len(path) == size:
            return near(first, path[-1], path[0])
        for nxt in range(size):
            if nxt not in path and near(first, path[-1], nxt):
                path.append(nxt)
                if extend():
                    return True
                path.pop()
        return False

    if not extend():
        return None
    for row in rows:
        if not all(near(row, path[j], path[(j + 1) % size]) for j in range(size)):
            return None
    return tuple(path)


def per_device(ring, latents, spatial_weight, temporal_weight, skip_weight, norm_gain, norm_bias):
    sections = lax.axis_size("segment")
    position = lax.axis_index("segment")
    steps_total = MICRO + sections - 1
    gains = norm_gain[0]
    offsets = norm_bias[0]
    width = spatial_weight.shape[-1]
    micro, samples, frames, rows, cols = latents.shape[:5]
    dims = (samples, frames, rows, cols)
    flat = latents.reshape(micro, -1, width)
    rs, rt = spatial_weight.shape[1], temporal_weight.shape[1]
    pack = jnp.concatenate([spatial_weight[0], temporal_weight[0], skip_weight[0]], axis=0)
    if ring is None:
        gathered = lax.all_gather(pack, "fsdp", axis=0, tiled=False)
    else:
        gathered = ring_gather(pack, "fsdp", ring)
    spatial3 = gathered[:, :rs].reshape(9, width, width)
    temporal3 = gathered[:, rs : rs + rt].reshape(3, width, width)
    skip_mat = gathered[:, rs + rt :].reshape(width, width)
    blank = jnp.zeros_like(flat[0])
    outputs = []
    skips = [None] * MICRO
    previous = blank
    pending = None
    for moment in range(steps_total):
        if moment == 0:
            stream = flat[0]
        else:
            pairs = [
                (s, s + 1) for s in range(sections - 1) if 0 <= moment - 1 - s < MICRO
            ]
            incoming = lax.ppermute(previous, "segment", pairs)
            sending = None
            if pending is not None:
                payload, incoming = lax.optimization_barrier((pending, incoming))
                sending = moment - 1
                skips[sending] = lax.ppermute(payload, "segment", [(0, sections - 1)])
                pending = None
            if moment < MICRO:
                stream = jnp.where(position == 0, flat[moment], incoming)
            else:
                stream = incoming
        late_index = moment - (sections - 1)
        skip_in = skips[late_index] if 0 <= late_index < MICRO else None
        output = section(stream, skip_in, spatial3, temporal3, skip_mat, gains, offsets, dims)
        if moment > 0 and sending is not None:
            skips[sending], output = lax.optimization_barrier((skips[sending], output))
        outputs.append(output)
        if moment < MICRO:
            pending = output
        previous = output
    held = lax.dynamic_slice_in_dim(jnp.stack(outputs), position, MICRO, axis=0)
    return held.reshape((1,) + latents.shape)


def solution(mesh):
    placed = (
        P(None, "fsdp", None, None, None, None),
        P("segment", "fsdp", None),
        P("segment", "fsdp", None),
        P("segment", "fsdp", None),
        P("segment", None, None),
        P("segment", None, None),
    )
    ring = neighbour_ring(mesh, "fsdp")
    return jax.shard_map(
        functools.partial(per_device, ring),
        mesh=mesh,
        in_specs=placed,
        out_specs=P("segment", None, "fsdp", None, None, None, None),
        check_vma=False,
    )
```

```python
import functools

import jax
import jax.numpy as jnp
from jax import lax
from jax.sharding import PartitionSpec as P

GROUPS = 32
MICRO = 2


precise = lax.Precision.HIGH


def group_norm(field, samples, gain, offset):
    width = field.shape[-1]
    grouped = field.reshape(samples, -1, GROUPS, width // GROUPS)
    center = jnp.mean(grouped, axis=(1, 3), keepdims=True)
    spread = jnp.mean((grouped - center) ** 2, axis=(1, 3), keepdims=True)
    normed = ((grouped - center) * lax.rsqrt(spread + 1e-05)).reshape(field.shape)
    return normed * gain + offset


def shifted(field, offset, valid, pad):
    padded = jnp.pad(field, ((pad, pad), (0, 0)))
    rows = field.shape[0]
    piece = padded[pad + offset : pad + offset + rows]
    return jnp.where(valid, piece, jnp.zeros_like(piece))


def spatial_conv(first, spatial3, frames, rows, cols):
    positions = first.shape[0]
    products = jnp.einsum(
        "pc,tco->tpo", first, spatial3, precision=precise, preferred_element_type=jnp.float32
    )
    pos = lax.broadcasted_iota(jnp.int32, (positions, 1), 0)
    within = pos % (rows * cols)
    row = within // cols
    col = within % cols
    total = None
    for delta_row in range(3):
        for delta_col in range(3):
            r = row + delta_row - 1
            c = col + delta_col - 1
            valid = (r >= 0) & (r < rows) & (c >= 0) & (c < cols)
            offset = (delta_row - 1) * cols + (delta_col - 1)
            piece = shifted(products[3 * delta_row + delta_col], offset, valid, cols + 1)
            total = piece if total is None else total + piece
    return total


def temporal_conv(second, temporal3, frames, rows, cols):
    positions = second.shape[0]
    plane = rows * cols
    products = jnp.einsum(
        "pc,tco->tpo", second, temporal3, precision=precise, preferred_element_type=jnp.float32
    )
    pos = lax.broadcasted_iota(jnp.int32, (positions, 1), 0)
    frame = (pos // plane) % frames
    total = None
    for tap in range(3):
        f = frame + tap - 1
        valid = (f >= 0) & (f < frames)
        piece = shifted(products[tap], (tap - 1) * plane, valid, plane)
        total = piece if total is None else total + piece
    return total


def section(x, skip_in, spatial3, temporal3, skip_mat, gains, offsets, dims):
    samples, frames, rows, cols = dims
    if skip_in is None:
        hidden = x
    else:
        hidden = x + jnp.dot(
            skip_in, skip_mat, precision=precise, preferred_element_type=jnp.float32
        )
    first = jax.nn.silu(group_norm(hidden, samples, gains[0], offsets[0]))
    mixed = hidden + spatial_conv(first, spatial3, frames, rows, cols)
    second = jax.nn.silu(group_norm(mixed, samples, gains[1], offsets[1]))
    return mixed + temporal_conv(second, temporal3, frames, rows, cols)


def ring_gather(pack, axis, ring):
    size = len(ring)
    place = [0] * size
    for spot, member in enumerate(ring):
        place[member] = spot
    me = lax.axis_index(axis)
    spot = jnp.array(place, jnp.int32)[me]
    members = jnp.array(ring, jnp.int32)
    out = jnp.zeros((size,) + pack.shape, pack.dtype)
    out = lax.dynamic_update_index_in_dim(out, pack, me, 0)
    ahead = [(ring[j], ring[(j + 1) % size]) for j in range(size)]
    behind = [(ring[(j + 1) % size], ring[j]) for j in range(size)]
    forward = backward = pack
    steps_forward = size // 2
    steps_backward = size - 1 - steps_forward
    for step in range(1, steps_forward + 1):
        forward = lax.ppermute(forward, axis, ahead)
        out = lax.dynamic_update_index_in_dim(out, forward, members[(spot - step) % size], 0)
        if step <= steps_backward:
            backward = lax.ppermute(backward, axis, behind)
            out = lax.dynamic_update_index_in_dim(
                out, backward, members[(spot + step) % size], 0
            )
    return out


def neighbour_ring(mesh, axis):
    names = list(mesh.axis_names)
    where = names.index(axis)
    grid = mesh.devices.transpose([i for i in range(len(names)) if i != where] + [where])
    rows = grid.reshape(-1, grid.shape[-1])
    size = rows.shape[1]
    if size < 3 or size > 16:
        return None

    def near(row, a, b):
        ca, cb = row[a].coords, row[b].coords
        return sum(abs(int(u) - int(v)) for u, v in zip(ca, cb)) == 1

    first = rows[0]
    path = [0]

    def extend():
        if len(path) == size:
            return near(first, path[-1], path[0])
        for nxt in range(size):
            if nxt not in path and near(first, path[-1], nxt):
                path.append(nxt)
                if extend():
                    return True
                path.pop()
        return False

    if not extend():
        return None
    for row in rows:
        if not all(near(row, path[j], path[(j + 1) % size]) for j in range(size)):
            return None
    return tuple(path)


def per_device(ring, latents, spatial_weight, temporal_weight, skip_weight, norm_gain, norm_bias):
    sections = lax.axis_size("segment")
    position = lax.axis_index("segment")
    steps_total = MICRO + sections - 1
    gains = norm_gain[0]
    offsets = norm_bias[0]
    width = spatial_weight.shape[-1]
    micro, samples, frames, rows, cols = latents.shape[:5]
    dims = (samples, frames, rows, cols)
    flat = latents.reshape(micro, -1, width)
    rs, rt = spatial_weight.shape[1], temporal_weight.shape[1]
    pack = jnp.concatenate([spatial_weight[0], temporal_weight[0], skip_weight[0]], axis=0)
    if ring is None:
        gathered = lax.all_gather(pack, "fsdp", axis=0, tiled=False)
    else:
        gathered = ring_gather(pack, "fsdp", ring)
    spatial3 = gathered[:, :rs].reshape(9, width, width)
    temporal3 = gathered[:, rs : rs + rt].reshape(3, width, width)
    skip_mat = gathered[:, rs + rt :].reshape(width, width)
    blank = jnp.zeros_like(flat[0])
    outputs = []
    skips = [None] * MICRO
    previous = blank
    pending = None
    for moment in range(steps_total):
        if moment == 0:
            stream = flat[0]
        else:
            pairs = [
                (s, s + 1) for s in range(sections - 1) if 0 <= moment - 1 - s < MICRO
            ]
            local = [(a, b) for a, b in pairs if a % 2 == 0]
            leaving = [(a, b) for a, b in pairs if a % 2 == 1]
            incoming = lax.ppermute(previous, "segment", local)
            half = (previous.shape[0] // 2 + 7) // 8 * 8
            for source, target in leaving:
                direct = lax.ppermute(previous[:half], "segment", [(source, target)])
                relay = lax.ppermute(previous[half:], "segment", [(source, source - 1)])
                relay = lax.ppermute(relay, "segment", [(source - 1, target)])
                whole = jnp.concatenate([direct, relay], axis=0)
                incoming = jnp.where(position == target, whole, incoming)
            sending = None
            if pending is not None:
                payload, incoming = lax.optimization_barrier((pending, incoming))
                sending = moment - 1
                skips[sending] = lax.ppermute(payload, "segment", [(0, sections - 1)])
                pending = None
            if moment < MICRO:
                stream = jnp.where(position == 0, flat[moment], incoming)
            else:
                stream = incoming
        late_index = moment - (sections - 1)
        skip_in = skips[late_index] if 0 <= late_index < MICRO else None
        output = section(stream, skip_in, spatial3, temporal3, skip_mat, gains, offsets, dims)
        if moment > 0 and sending is not None:
            skips[sending], output = lax.optimization_barrier((skips[sending], output))
        outputs.append(output)
        if moment < MICRO:
            pending = output
        previous = output
    held = lax.dynamic_slice_in_dim(jnp.stack(outputs), position, MICRO, axis=0)
    return held.reshape((1,) + latents.shape)


def solution(mesh):
    placed = (
        P(None, "fsdp", None, None, None, None),
        P("segment", "fsdp", None),
        P("segment", "fsdp", None),
        P("segment", "fsdp", None),
        P("segment", None, None),
        P("segment", None, None),
    )
    ring = neighbour_ring(mesh, "fsdp")
    return jax.shard_map(
        functools.partial(per_device, ring),
        mesh=mesh,
        in_specs=placed,
        out_specs=P("segment", None, "fsdp", None, None, None, None),
        check_vma=False,
    )
```

```python
import functools

import jax
import jax.numpy as jnp
from jax import lax
from jax.sharding import PartitionSpec as P

GROUPS = 32
MICRO = 2


precise = lax.Precision.HIGH


def group_norm(field, samples, gain, offset):
    width = field.shape[-1]
    grouped = field.reshape(samples, -1, GROUPS, width // GROUPS)
    center = jnp.mean(grouped, axis=(1, 3), keepdims=True)
    spread = jnp.mean((grouped - center) ** 2, axis=(1, 3), keepdims=True)
    normed = ((grouped - center) * lax.rsqrt(spread + 1e-05)).reshape(field.shape)
    return normed * gain + offset


def shifted(field, offset, valid, pad):
    padded = jnp.pad(field, ((pad, pad), (0, 0)))
    rows = field.shape[0]
    piece = padded[pad + offset : pad + offset + rows]
    return jnp.where(valid, piece, jnp.zeros_like(piece))


def spatial_conv(first, spatial3, frames, rows, cols):
    positions = first.shape[0]
    products = jnp.einsum(
        "pc,tco->tpo", first, spatial3, precision=precise, preferred_element_type=jnp.float32
    )
    pos = lax.broadcasted_iota(jnp.int32, (positions, 1), 0)
    within = pos % (rows * cols)
    row = within // cols
    col = within % cols
    total = None
    for delta_row in range(3):
        for delta_col in range(3):
            r = row + delta_row - 1
            c = col + delta_col - 1
            valid = (r >= 0) & (r < rows) & (c >= 0) & (c < cols)
            offset = (delta_row - 1) * cols + (delta_col - 1)
            piece = shifted(products[3 * delta_row + delta_col], offset, valid, cols + 1)
            total = piece if total is None else total + piece
    return total


def temporal_conv(second, temporal3, frames, rows, cols):
    positions = second.shape[0]
    plane = rows * cols
    products = jnp.einsum(
        "pc,tco->tpo", second, temporal3, precision=precise, preferred_element_type=jnp.float32
    )
    pos = lax.broadcasted_iota(jnp.int32, (positions, 1), 0)
    frame = (pos // plane) % frames
    total = None
    for tap in range(3):
        f = frame + tap - 1
        valid = (f >= 0) & (f < frames)
        piece = shifted(products[tap], (tap - 1) * plane, valid, plane)
        total = piece if total is None else total + piece
    return total


def section(x, skip_in, spatial3, temporal3, skip_mat, gains, offsets, dims):
    samples, frames, rows, cols = dims
    if skip_in is None:
        hidden = x
    else:
        hidden = x + jnp.dot(
            skip_in, skip_mat, precision=precise, preferred_element_type=jnp.float32
        )
    first = jax.nn.silu(group_norm(hidden, samples, gains[0], offsets[0]))
    mixed = hidden + spatial_conv(first, spatial3, frames, rows, cols)
    second = jax.nn.silu(group_norm(mixed, samples, gains[1], offsets[1]))
    return mixed + temporal_conv(second, temporal3, frames, rows, cols)


def ring_gather(pack, axis, ring):
    size = len(ring)
    place = [0] * size
    for spot, member in enumerate(ring):
        place[member] = spot
    me = lax.axis_index(axis)
    spot = jnp.array(place, jnp.int32)[me]
    members = jnp.array(ring, jnp.int32)
    out = jnp.zeros((size,) + pack.shape, pack.dtype)
    out = lax.dynamic_update_index_in_dim(out, pack, me, 0)
    ahead = [(ring[j], ring[(j + 1) % size]) for j in range(size)]
    behind = [(ring[(j + 1) % size], ring[j]) for j in range(size)]
    forward = backward = pack
    steps_forward = size // 2
    steps_backward = size - 1 - steps_forward
    for step in range(1, steps_forward + 1):
        forward = lax.ppermute(forward, axis, ahead)
        out = lax.dynamic_update_index_in_dim(out, forward, members[(spot - step) % size], 0)
        if step <= steps_backward:
            backward = lax.ppermute(backward, axis, behind)
            out = lax.dynamic_update_index_in_dim(
                out, backward, members[(spot + step) % size], 0
            )
    return out


def neighbour_ring(mesh, axis):
    names = list(mesh.axis_names)
    where = names.index(axis)
    grid = mesh.devices.transpose([i for i in range(len(names)) if i != where] + [where])
    rows = grid.reshape(-1, grid.shape[-1])
    size = rows.shape[1]
    if size < 3 or size > 16:
        return None

    def near(row, a, b):
        ca, cb = row[a].coords, row[b].coords
        return sum(abs(int(u) - int(v)) for u, v in zip(ca, cb)) == 1

    first = rows[0]
    path = [0]

    def extend():
        if len(path) == size:
            return near(first, path[-1], path[0])
        for nxt in range(size):
            if nxt not in path and near(first, path[-1], nxt):
                path.append(nxt)
                if extend():
                    return True
                path.pop()
        return False

    if not extend():
        return None
    for row in rows:
        if not all(near(row, path[j], path[(j + 1) % size]) for j in range(size)):
            return None
    return tuple(path)


def per_device(ring, latents, spatial_weight, temporal_weight, skip_weight, norm_gain, norm_bias):
    sections = lax.axis_size("segment")
    position = lax.axis_index("segment")
    steps_total = MICRO + sections - 1
    gains = norm_gain[0]
    offsets = norm_bias[0]
    width = spatial_weight.shape[-1]
    micro, samples, frames, rows, cols = latents.shape[:5]
    dims = (samples, frames, rows, cols)
    flat = latents.reshape(micro, -1, width)
    rs, rt = spatial_weight.shape[1], temporal_weight.shape[1]
    pack = jnp.concatenate([spatial_weight[0], temporal_weight[0], skip_weight[0]], axis=0)
    if ring is None:
        gathered = lax.all_gather(pack, "fsdp", axis=0, tiled=False)
    else:
        gathered = ring_gather(pack, "fsdp", ring)
    spatial3 = gathered[:, :rs].reshape(9, width, width)
    temporal3 = gathered[:, rs : rs + rt].reshape(3, width, width)
    skip_mat = gathered[:, rs + rt :].reshape(width, width)
    blank = jnp.zeros_like(flat[0])
    outputs = []
    skips = [None] * MICRO
    previous = blank
    pending = None
    for moment in range(steps_total):
        if moment == 0:
            stream = flat[0]
        else:
            pairs = [
                (s, s + 1) for s in range(sections - 1) if 0 <= moment - 1 - s < MICRO
            ]
            incoming = lax.ppermute(previous, "segment", pairs)
            stored, incoming = lax.optimization_barrier((outputs[-1], incoming))
            outputs[-1] = stored
            sending = None
            if pending is not None:
                payload, incoming = lax.optimization_barrier((pending, incoming))
                sending = moment - 1
                skips[sending] = lax.ppermute(payload, "segment", [(0, sections - 1)])
                pending = None
            if moment < MICRO:
                stream = jnp.where(position == 0, flat[moment], incoming)
            else:
                stream = incoming
        late_index = moment - (sections - 1)
        skip_in = skips[late_index] if 0 <= late_index < MICRO else None
        output = section(stream, skip_in, spatial3, temporal3, skip_mat, gains, offsets, dims)
        if moment > 0 and sending is not None:
            skips[sending], output = lax.optimization_barrier((skips[sending], output))
        outputs.append(output)
        if moment < MICRO:
            pending = output
        previous = output
    held = lax.dynamic_slice_in_dim(jnp.stack(outputs), position, MICRO, axis=0)
    return held.reshape((1,) + latents.shape)


def solution(mesh):
    placed = (
        P(None, "fsdp", None, None, None, None),
        P("segment", "fsdp", None),
        P("segment", "fsdp", None),
        P("segment", "fsdp", None),
        P("segment", None, None),
        P("segment", None, None),
    )
    ring = neighbour_ring(mesh, "fsdp")
    return jax.shard_map(
        functools.partial(per_device, ring),
        mesh=mesh,
        in_specs=placed,
        out_specs=P("segment", None, "fsdp", None, None, None, None),
        check_vma=False,
    )
```
